32 devices in a mesh: tile: 8 (over z, x), pred: 4 (over y, core).
Axes of the slice: x: 2, y: 2, z: 4, core: 2. Of those that a mesh axis runs over, the one named last changes fastest.
Arguments:
- covariates: bfloat16 [64, 1024, 8192], P('pred', 'tile'), may hold values from -1.5 to 1.5
- target: float32 [1024, 8192], P('tile'), may hold values from -6 to 6
- land: int32 [1024, 8192], P('tile'), may hold values 0 or 1
- coefs: float32 [64, 64, 512], P('pred', 'tile'), may hold values from -6 to 6
- first_moment: float32 [64, 64, 512], P('pred', 'tile'), may hold values from -3 to 3
- second_moment: float32 [64, 64, 512], P('pred', 'tile'), may hold values from 0.05 to 1
- smoothing: float32 [64], P('pred'), may hold values from 0.01 to 0.1
Outputs:
- fitted: float32 [1024, 8192], P(('tile', 'pred'))
- residual: float32 [1024, 8192], P(('tile', 'pred'))
- gradient: float32 [64, 64, 512], P('pred', 'tile')
- new_coefs: float32 [64, 64, 512], P('pred', 'tile')
- new_first: float32 [64, 64, 512], P('pred', 'tile')
- new_second: float32 [64, 64, 512], P('pred', 'tile')
The draws below stay inside these ranges and needn't reach their ends.
Inputs may be any that keep to these rules, and one draw needn't show every extreme that they name: land is 1 on land cells and 0 elsewhere.
All inputs are finite; a program needn't handle non-finite values. No bound on the sum of `land` on one device may be relied on, other than what follows from the above.
Results may differ from the reference program's by a relative error of at most 0.0003.
Values sent between devices are 32-bit elements; how exact they have to be, the bound alone decides.
No kernel may reach another device: no remote copies, remote signals or barrier semaphores. Data moves between devices by JAX's collectives and lax.ppermute only.
A program may use at most 128 MiB of HBM per device.

```python
import math
import jax
import jax.numpy as jnp
from jax import lax

SURFACES = 64
KY = 512
H = 16
KX = 64
NX = 1024
NY = 8192


def plant(values, stream_key, smallest, top_value):
    spot = [jax.random.randint(jax.random.fold_in(stream_key, axis), (), 0, length) for axis, length in enumerate(values.shape)]
    widest = values.shape.index(max(values.shape))
    next_to = spot[:widest] + [(spot[widest] + 1) % values.shape[widest]] + spot[widest + 1:]
    return values.at[tuple(spot)].set(smallest).at[tuple(next_to)].set(top_value)


def level_of(own_key, shape, cuts, least, high):
    factor_of = 1.0
    for axis_at, shards_of in cuts:
        steps = jax.random.uniform(jax.random.fold_in(jax.random.fold_in(own_key, 6), axis_at), (shards_of,), jnp.float32, least / len(cuts), high / len(cuts))
        factor_of = factor_of * jnp.repeat(jnp.exp(steps), shape[axis_at] // shards_of).reshape((-1,) + (1,) * (len(shape) - 1 - axis_at))
    return factor_of


def normal_values(rng, dims, scale, reach, shards=(), kind=jnp.bfloat16):
    loudness = level_of(rng, dims, shards, -0.22, 0.18) if shards else 1.0
    values = jax.random.normal(rng, dims, jnp.float32) * scale * loudness
    return jnp.minimum(jnp.maximum(values, -reach), reach).astype(kind)


def setup_inputs(seed: int = 0) -> dict:
    seeds = jax.random.split(jax.random.key(seed), 8)
    return {
        "covariates": normal_values(seeds[0], (SURFACES, NX, NY), 0.25, 1.5, ((0, 4), (1, 8))),
        "target": normal_values(seeds[1], (NX, NY), 1.0, 6.0, ((0, 8),), jnp.float32),
        "land": plant((jax.random.randint(seeds[2], (NX, NY), 0, 5) < 4).astype(jnp.int32), jax.random.fold_in(seeds[2], 1), 0, 1),
        "coefs": normal_values(seeds[3], (SURFACES, KX, KY), 1.0, 6.0, ((0, 4), (1, 8)), jnp.float32),
        "first_moment": normal_values(seeds[4], (SURFACES, KX, KY), 0.2, 3.0, ((0, 4), (1, 8)), jnp.float32),
        "second_moment": jnp.clip(jnp.exp(math.log(1.0) - 2.9957323 * jax.random.uniform(seeds[5], (SURFACES, KX, KY), jnp.float32) ** level_of(seeds[5], (SURFACES, KX, KY), ((0, 4), (1, 8)), -0.2, 0.2)), 0.05, 1.0),
        "smoothing": jnp.clip(jnp.exp(math.log(0.1) - 2.3025851 * jax.random.uniform(seeds[6], (SURFACES,), jnp.float32) ** level_of(seeds[6], (SURFACES,), ((0, 4),), -0.2, 0.2)), 0.01, 0.1),
    }


def weights_of(u):
    return [(1.0 - u) * (1.0 - u) * (1.0 - u) / 6.0, (3.0 * u * u * u - 6.0 * u * u + 4.0) / 6.0, (-3.0 * u * u * u + 3.0 * u * u + 3.0 * u + 1.0) / 6.0, u * u * u / 6.0]

def weight_table(spacing):
    u = (jnp.arange(spacing, dtype=jnp.float32) + 0.5) / spacing
    return jnp.stack(weights_of(u))

def column_basis(knots, spacing):
    cells = jnp.arange(knots * spacing, dtype=jnp.int32)
    interval = cells // spacing
    u = ((cells % spacing).astype(jnp.float32) + 0.5) / spacing
    values = weights_of(u)
    offset = jnp.arange(knots, dtype=jnp.int32)[:, None] - interval[None, :] + 1
    basis = jnp.zeros((knots, knots * spacing), jnp.float32)
    for dd in range(4):
        basis = jnp.where(offset == dd, values[dd][None, :], basis)
    return basis

def spread(padded, table, count, offset):
    spacing = table.shape[1]
    total = None
    for dd in range(4):
        rows = padded[..., offset + dd:offset + dd + count, :]
        term = table[dd][:, None] * rows[..., :, None, :]
        total = term if total is None else total + term
    return total.reshape(padded.shape[:-2] + (count * spacing, padded.shape[-1]))

def collect(field, table, count, lead):
    spacing = table.shape[1]
    shaped = field.reshape(field.shape[:-2] + (count, spacing, field.shape[-1]))
    total = None
    for dd in range(4):
        term = lax.optimization_barrier(jnp.sum(shaped * table[dd][:, None], axis=-2))
        widths = [(0, 0)] * (term.ndim - 2) + [(lead + dd, 3 - dd), (0, 0)]
        term = jnp.pad(term, widths)
        total = term if total is None else total + term
    return total

def penalty(padded, count):
    stencil = [1.0, -4.0, 6.0, -4.0, 1.0]
    along_rows = None
    for ii in range(5):
        term = stencil[ii] * padded[..., ii:ii + count, :]
        along_rows = term if along_rows is None else along_rows + term
    centre = padded[..., 2:count + 2, :]
    width = centre.shape[-1]
    wide = jnp.pad(centre, [(0, 0)] * (centre.ndim - 1) + [(2, 2)])
    for ii in range(5):
        along_rows = along_rows + stencil[ii] * wide[..., ii:ii + width]
    return along_rows

def reference(covariates, target, land, coefs, first_moment, second_moment, smoothing):
    table = weight_table(H)
    basis = column_basis(KY, H)
    count = coefs.shape[1]

    def add_surface(total, pair):
        cover, coef = pair
        along = jnp.dot(coef, basis, precision=lax.Precision.HIGHEST)
        surface = spread(jnp.pad(along, ((1, 2), (0, 0))), table, count, 0)
        return (total + cover.astype(jnp.float32) * surface, None)
    fitted, unused = lax.scan(add_surface, jnp.zeros(target.shape, jnp.float32), (covariates, coefs))
    residual = land.astype(jnp.float32) * (target - fitted)

    def one_gradient(triple):
        cover, coef, weight = triple
        back = collect(residual * cover.astype(jnp.float32), table, count, 0)[1:count + 1]
        data = -(1.0 / H) * jnp.dot(back, basis.T, precision=lax.Precision.HIGHEST)
        return data + weight * penalty(jnp.pad(coef, ((2, 2), (0, 0))), count)
    gradient = lax.map(one_gradient, (covariates, coefs, smoothing))
    new_first = 0.9 * first_moment + 0.1 * gradient
    new_second = 0.99 * second_moment + 0.01 * gradient * gradient
    new_coefs = coefs - 0.1 * new_first / (jnp.sqrt(new_second) + 1e-08)
    return (fitted, residual, gradient, new_coefs, new_first, new_second)
```

```python
import jax
import jax.numpy as jnp
from jax import lax
from jax.experimental import pallas as pl
from jax.experimental.pallas import tpu as pltpu
from jax.sharding import PartitionSpec as P

H = 16
TN = 512
L = 256
CHUNKS = 4
LEAD = 8


def extended(array, sides, width):
    for axis, dim in sides:
        peers, length = (lax.axis_size(axis), array.shape[dim])
        up = [(i, (i + 1) % peers) for i in range(peers - 1)]
        down = [(j, i) for i, j in up]
        last = lax.slice_in_dim(array, length - width, length, axis=dim)
        first = lax.slice_in_dim(array, 0, width, axis=dim)
        before = lax.ppermute(last, axis, up)
        after = lax.ppermute(first, axis, down)
        array = jnp.concatenate([before, array, after], axis=dim)
    return array


def from_behind(block, axis, distance):
    devices = range(lax.axis_size(axis))
    route = [(i - distance, i) for i in devices if i - distance in devices]
    return lax.ppermute(block, axis, route)


def weights_of(u):
    return [
        (1.0 - u) * (1.0 - u) * (1.0 - u) / 6.0,
        (3.0 * u * u * u - 6.0 * u * u + 4.0) / 6.0,
        (-3.0 * u * u * u + 3.0 * u * u + 3.0 * u + 1.0) / 6.0,
        u * u * u / 6.0,
    ]


def weight_table(spacing):
    u = (jnp.arange(spacing, dtype=jnp.float32) + 0.5) / spacing
    return jnp.stack(weights_of(u))


def block_basis(window):
    n = jnp.arange(window, dtype=jnp.int32)[:, None]
    j = jnp.arange(TN, dtype=jnp.int32)[None, :]
    u = ((j % H).astype(jnp.float32) + 0.5) / H
    values = weights_of(u)
    offset = n - LEAD + 1 - j // H
    basis = jnp.zeros((window, TN), jnp.float32)
    for dd in range(4):
        basis = jnp.where(offset == dd, values[dd], basis)
    return basis


def banded_along(padded, ny):
    knots = padded.shape[-1]
    per_block = TN // H
    window = 4 * per_block
    blocks = ny // TN
    right = per_block * (blocks - 1) + window - knots - LEAD
    cpad = jnp.pad(padded, ((0, 0), (0, 0), (LEAD, right)))
    cwin = jnp.stack([cpad[..., per_block * b : per_block * b + window] for b in range(blocks)], axis=2)
    along = jnp.einsum("pkbn,nj->pkbj", cwin, block_basis(window), precision=lax.Precision.HIGHEST)
    return along.reshape(padded.shape[:2] + (ny,))


def banded_data(back, knots):
    npred, nrow, ny = back.shape
    per_block = TN // H
    window = 4 * per_block
    blocks = ny // TN
    back4 = back.reshape(npred, nrow, blocks, TN)
    dwin = jnp.einsum("pkbj,nj->pkbn", back4, block_basis(window), precision=lax.Precision.HIGHEST)
    total = None
    for a in range(4):
        part = dwin[..., a * per_block : (a + 1) * per_block]
        part = jnp.pad(part, ((0, 0), (0, 0), (a, 3 - a), (0, 0)))
        total = part if total is None else total + part
    total = total.reshape(npred, nrow, (blocks + 3) * per_block)
    return total[..., LEAD : LEAD + knots]


def fit_kernel(w_ref, cov_ref, a_ref, o_ref):
    npred = cov_ref.shape[0]
    nint = cov_ref.shape[1] // H
    for s in range(TN // L):
        cols = pl.ds(s * L, L)
        w = [w_ref[d] for d in range(4)]
        for m in range(nint):
            rows = pl.ds(m * H, H)

            def body(p, acc):
                surf = w[0] * a_ref[p, pl.ds(m + 1, 1), cols]
                for d in range(1, 4):
                    surf = surf + w[d] * a_ref[p, pl.ds(m + 1 + d, 1), cols]
                return acc + cov_ref[p, rows, cols].astype(jnp.float32) * surf

            acc = lax.fori_loop(0, npred, body, jnp.zeros((H, L), jnp.float32), unroll=True)
            o_ref[rows, cols] = acc


def back_kernel(w_ref, cov_ref, r_ref, o_ref, rw_ref):
    npred = cov_ref.shape[0]
    nint = cov_ref.shape[1] // H
    for s in range(TN // L):
        cols = pl.ds(s * L, L)
        for d in range(4):
            for m in range(nint):
                rw_ref[d, pl.ds(m * H, H), :] = w_ref[d] * r_ref[pl.ds(m * H, H), cols]

        def body(p, carry):
            o_ref[p, pl.ds(0, 1), cols] = jnp.zeros((1, L), jnp.float32)
            accs = {}
            for m in range(nint):
                c = cov_ref[p, pl.ds(m * H, H), cols].astype(jnp.float32)
                for d in range(4):
                    prod = c * rw_ref[d, pl.ds(m * H, H), :]
                    half = prod[0:8] + prod[8:16]
                    r = m + 1 + d
                    accs[r] = half if r not in accs else accs[r] + half
                done = m + 1
                o_ref[p, pl.ds(done, 1), cols] = jnp.sum(accs.pop(done), axis=0, keepdims=True)
            for r in sorted(accs):
                o_ref[p, pl.ds(r, 1), cols] = jnp.sum(accs[r], axis=0, keepdims=True)
            return carry

        lax.fori_loop(0, npred, body, 0)


def fit_chunk(wl, cov, along, chunk, width):
    npred, rows, _ = cov.shape
    nrow = along.shape[1]
    off = chunk * (width // TN)
    return pl.pallas_call(
        fit_kernel,
        grid=(width // TN,),
        in_specs=[
            pl.BlockSpec((4, H, L), lambda j: (0, 0, 0)),
            pl.BlockSpec((npred, rows, TN), lambda j: (0, 0, j + off)),
            pl.BlockSpec((npred, nrow, TN), lambda j: (0, 0, j + off)),
        ],
        out_specs=pl.BlockSpec((rows, TN), lambda j: (0, j)),
        out_shape=jax.ShapeDtypeStruct((rows, width), jnp.float32),
        compiler_params=pltpu.CompilerParams(dimension_semantics=("arbitrary",)),
    )(wl, cov, along)


def back_chunk(wl, cov, resid, chunk, nrow):
    npred, rows, _ = cov.shape
    width = resid.shape[1]
    off = chunk * (width // TN)
    return pl.pallas_call(
        back_kernel,
        grid=(width // TN,),
        in_specs=[
            pl.BlockSpec((4, H, L), lambda j: (0, 0, 0)),
            pl.BlockSpec((npred, rows, TN), lambda j: (0, 0, j + off)),
            pl.BlockSpec((rows, TN), lambda j: (0, j)),
        ],
        out_specs=pl.BlockSpec((npred, nrow, TN), lambda j: (0, 0, j)),
        out_shape=jax.ShapeDtypeStruct((npred, nrow, width), jnp.float32),
        scratch_shapes=[pltpu.VMEM((4, rows, L), jnp.float32)],
        compiler_params=pltpu.CompilerParams(dimension_semantics=("arbitrary",)),
    )(wl, cov, resid)


def penalty(padded, count):
    stencil = [1.0, -4.0, 6.0, -4.0, 1.0]
    along_rows = None
    for ii in range(5):
        term = stencil[ii] * padded[..., ii : ii + count, :]
        along_rows = term if along_rows is None else along_rows + term
    centre = padded[..., 2 : count + 2, :]
    width = centre.shape[-1]
    wide = jnp.pad(centre, [(0, 0)] * (centre.ndim - 1) + [(2, 2)])
    for ii in range(5):
        along_rows = along_rows + stencil[ii] * wide[..., ii : ii + width]
    return along_rows


def local(covariates, target, land, coefs, first_moment, second_moment, smoothing):
    npred, rows, ny = covariates.shape
    count = coefs.shape[1]
    knots = coefs.shape[2]
    share = rows // lax.axis_size("pred")
    start = lax.axis_index("pred") * share
    wl = jnp.broadcast_to(weight_table(H)[:, :, None], (4, H, L))
    padded = extended(coefs, (("tile", 1),), 2)
    along = banded_along(padded, ny)
    nrow = padded.shape[1]
    target_blk = lax.dynamic_slice_in_dim(target, start, share, 0)
    land_blk = lax.dynamic_slice_in_dim(land, start, share, 0).astype(jnp.float32)
    width = ny // CHUNKS
    fitted_parts, resid_parts, back_parts = [], [], []
    for c in range(CHUNKS):
        partial = fit_chunk(wl, covariates, along, c, width)
        fitted_c = lax.psum_scatter(partial, "pred", scatter_dimension=0, tiled=True)
        cols = slice(c * width, (c + 1) * width)
        resid_c = land_blk[:, cols] * (target_blk[:, cols] - fitted_c)
        resid_full = lax.all_gather(resid_c, "pred", axis=0, tiled=True)
        back_parts.append(back_chunk(wl, covariates, resid_full, c, nrow))
        fitted_parts.append(fitted_c)
        resid_parts.append(resid_c)
    fitted = jnp.concatenate(fitted_parts, axis=1)
    residual = jnp.concatenate(resid_parts, axis=1)
    back = jnp.concatenate(back_parts, axis=2)
    grad_pad = -(1.0 / H) * banded_data(back, knots)
    inner = grad_pad[:, 2 : count + 2]
    from_below = from_behind(grad_pad[:, count + 2 :], "tile", 1)
    from_above = from_behind(grad_pad[:, :2], "tile", -1)
    middle = jnp.zeros((inner.shape[0], count - 2, inner.shape[2]), jnp.float32)
    low_add = jnp.concatenate([from_below, middle], axis=1)
    high_add = jnp.concatenate([middle, from_above], axis=1)
    data = inner + low_add + high_add
    gradient = data + smoothing[:, None, None] * penalty(padded, count)
    new_first = 0.9 * first_moment + 0.1 * gradient
    new_second = 0.99 * second_moment + 0.01 * gradient * gradient
    new_coefs = coefs - 0.1 * new_first / (jnp.sqrt(new_second) + 1e-08)
    return (fitted, residual, gradient, new_coefs, new_first, new_second)


def solution(mesh):
    in_specs = (
        P("pred", "tile", None),
        P("tile", None),
        P("tile", None),
        P("pred", "tile", None),
        P("pred", "tile", None),
        P("pred", "tile", None),
        P("pred"),
    )
    out_specs = (
        P(("tile", "pred"), None),
        P(("tile", "pred"), None),
        P("pred", "tile", None),
        P("pred", "tile", None),
        P("pred", "tile", None),
        P("pred", "tile", None),
    )
    return jax.shard_map(local, mesh=mesh, in_specs=in_specs, out_specs=out_specs, check_vma=False)
```

```python
import jax
import jax.numpy as jnp
from jax import lax
from jax.experimental import pallas as pl
from jax.experimental.pallas import tpu as pltpu
from jax.sharding import PartitionSpec as P

H = 16
TN = 512
L = 256
CHUNKS = 4
LEAD = 8


def extended(array, sides, width):
    for axis, dim in sides:
        peers, length = (lax.axis_size(axis), array.shape[dim])
        up = [(i, (i + 1) % peers) for i in range(peers - 1)]
        down = [(j, i) for i, j in up]
        last = lax.slice_in_dim(array, length - width, length, axis=dim)
        first = lax.slice_in_dim(array, 0, width, axis=dim)
        before = lax.ppermute(last, axis, up)
        after = lax.ppermute(first, axis, down)
        array = jnp.concatenate([before, array, after], axis=dim)
    return array


def from_behind(block, axis, distance):
    devices = range(lax.axis_size(axis))
    route = [(i - distance, i) for i in devices if i - distance in devices]
    return lax.ppermute(block, axis, route)


def weights_of(u):
    return [
        (1.0 - u) * (1.0 - u) * (1.0 - u) / 6.0,
        (3.0 * u * u * u - 6.0 * u * u + 4.0) / 6.0,
        (-3.0 * u * u * u + 3.0 * u * u + 3.0 * u + 1.0) / 6.0,
        u * u * u / 6.0,
    ]


def weight_table(spacing):
    u = (jnp.arange(spacing, dtype=jnp.float32) + 0.5) / spacing
    return jnp.stack(weights_of(u))


def block_basis(window):
    n = jnp.arange(window, dtype=jnp.int32)[:, None]
    j = jnp.arange(TN, dtype=jnp.int32)[None, :]
    u = ((j % H).astype(jnp.float32) + 0.5) / H
    values = weights_of(u)
    offset = n - LEAD + 1 - j // H
    basis = jnp.zeros((window, TN), jnp.float32)
    for dd in range(4):
        basis = jnp.where(offset == dd, values[dd], basis)
    return basis


def banded_along(padded, ny):
    knots = padded.shape[-1]
    per_block = TN // H
    window = 4 * per_block
    blocks = ny // TN
    right = per_block * (blocks - 1) + window - knots - LEAD
    cpad = jnp.pad(padded, ((0, 0), (0, 0), (LEAD, right)))
    cwin = jnp.stack([cpad[..., per_block * b : per_block * b + window] for b in range(blocks)], axis=1)
    return jnp.einsum("pbkn,nj->pbkj", cwin, block_basis(window), precision=lax.Precision.HIGHEST)


def banded_data(back4, knots):
    npred, blocks, nrow, _ = back4.shape
    per_block = TN // H
    window = 4 * per_block
    dwin = jnp.einsum("pbkj,nj->pkbn", back4, block_basis(window), precision=lax.Precision.HIGHEST)
    total = None
    for a in range(4):
        part = dwin[..., a * per_block : (a + 1) * per_block]
        part = jnp.pad(part, ((0, 0), (0, 0), (a, 3 - a), (0, 0)))
        total = part if total is None else total + part
    total = total.reshape(npred, nrow, (blocks + 3) * per_block)
    return total[..., LEAD : LEAD + knots]


def allreduce_rows(x, axis):
    n = lax.axis_size(axis)
    idx = lax.axis_index(axis)
    bits = []
    bit = 1
    while bit < n:
        bits.append(bit)
        bit *= 2
    cur = x
    for bit in bits:
        half = cur.shape[0] // 2
        mine = (idx // bit) % 2
        pair = cur.reshape((2, half) + cur.shape[1:])
        keep = lax.dynamic_index_in_dim(pair, mine, 0, keepdims=False)
        send = lax.dynamic_index_in_dim(pair, 1 - mine, 0, keepdims=False)
        cur = keep + lax.ppermute(send, axis, [(i, i ^ bit) for i in range(n)])
    for bit in reversed(bits):
        mine = (idx // bit) % 2
        other = lax.ppermute(cur, axis, [(i, i ^ bit) for i in range(n)])
        first = jnp.where(mine == 0, cur, other)
        second = jnp.where(mine == 0, other, cur)
        cur = jnp.concatenate([first, second], axis=0)
    return cur


def fit_kernel(w_ref, cov_ref, a_ref, o_ref):
    npred = cov_ref.shape[0]
    nint = cov_ref.shape[1] // H
    for s in range(TN // L):
        cols = pl.ds(s * L, L)
        w = [w_ref[d] for d in range(4)]
        for m in range(nint):
            rows = pl.ds(m * H, H)

            def body(p, acc):
                surf = w[0] * a_ref[p, 0, pl.ds(m + 1, 1), cols]
                for d in range(1, 4):
                    surf = surf + w[d] * a_ref[p, 0, pl.ds(m + 1 + d, 1), cols]
                return acc + cov_ref[p, rows, cols].astype(jnp.float32) * surf

            acc = lax.fori_loop(0, npred, body, jnp.zeros((H, L), jnp.float32), unroll=True)
            o_ref[rows, cols] = acc


def back_kernel(w_ref, cov_ref, t_ref, y_ref, g_ref, o_ref, rw_ref):
    npred = cov_ref.shape[0]
    nint = cov_ref.shape[1] // H
    for s in range(TN // L):
        cols = pl.ds(s * L, L)
        for m in range(nint):
            rows = pl.ds(m * H, H)
            resid = g_ref[rows, cols].astype(jnp.float32) * (y_ref[rows, cols] - t_ref[rows, cols])
            for d in range(4):
                rw_ref[d, rows, :] = w_ref[d] * resid

        def body(p, carry):
            o_ref[p, 0, pl.ds(0, 1), cols] = jnp.zeros((1, L), jnp.float32)
            accs = {}
            for m in range(nint):
                c = cov_ref[p, pl.ds(m * H, H), cols].astype(jnp.float32)
                for d in range(4):
                    prod = c * rw_ref[d, pl.ds(m * H, H), :]
                    half = prod[0:8] + prod[8:16]
                    r = m + 1 + d
                    accs[r] = half if r not in accs else accs[r] + half
                done = m + 1
                o_ref[p, 0, pl.ds(done, 1), cols] = jnp.sum(accs.pop(done), axis=0, keepdims=True)
            for r in sorted(accs):
                o_ref[p, 0, pl.ds(r, 1), cols] = jnp.sum(accs[r], axis=0, keepdims=True)
            return carry

        lax.fori_loop(0, npred, body, 0)


def fit_chunk(wl, cov, along, chunk, width):
    npred, rows, _ = cov.shape
    nrow = along.shape[2]
    off = chunk * (width // TN)
    return pl.pallas_call(
        fit_kernel,
        grid=(width // TN,),
        in_specs=[
            pl.BlockSpec((4, H, L), lambda j: (0, 0, 0)),
            pl.BlockSpec((npred, rows, TN), lambda j: (0, 0, j + off)),
            pl.BlockSpec((npred, 1, nrow, TN), lambda j: (0, j + off, 0, 0)),
        ],
        out_specs=pl.BlockSpec((rows, TN), lambda j: (0, j)),
        out_shape=jax.ShapeDtypeStruct((rows, width), jnp.float32),
        compiler_params=pltpu.CompilerParams(dimension_semantics=("arbitrary",)),
    )(wl, cov, along)


def back_chunk(wl, cov, total, target, land, chunk, nrow):
    npred, rows, _ = cov.shape
    width = total.shape[1]
    off = chunk * (width // TN)
    return pl.pallas_call(
        back_kernel,
        grid=(width // TN,),
        in_specs=[
            pl.BlockSpec((4, H, L), lambda j: (0, 0, 0)),
            pl.BlockSpec((npred, rows, TN), lambda j: (0, 0, j + off)),
            pl.BlockSpec((rows, TN), lambda j: (0, j)),
            pl.BlockSpec((rows, TN), lambda j: (0, j + off)),
            pl.BlockSpec((rows, TN), lambda j: (0, j + off)),
        ],
        out_specs=pl.BlockSpec((npred, 1, nrow, TN), lambda j: (0, j, 0, 0)),
        out_shape=jax.ShapeDtypeStruct((npred, width // TN, nrow, TN), jnp.float32),
        scratch_shapes=[pltpu.VMEM((4, rows, L), jnp.float32)],
        compiler_params=pltpu.CompilerParams(dimension_semantics=("arbitrary",)),
    )(wl, cov, total, target, land)


def penalty(padded, count):
    stencil = [1.0, -4.0, 6.0, -4.0, 1.0]
    along_rows = None
    for ii in range(5):
        term = stencil[ii] * padded[..., ii : ii + count, :]
        along_rows = term if along_rows is None else along_rows + term
    centre = padded[..., 2 : count + 2, :]
    width = centre.shape[-1]
    wide = jnp.pad(centre, [(0, 0)] * (centre.ndim - 1) + [(2, 2)])
    for ii in range(5):
        along_rows = along_rows + stencil[ii] * wide[..., ii : ii + width]
    return along_rows


def local(covariates, target, land, coefs, first_moment, second_moment, smoothing):
    npred, rows, ny = covariates.shape
    count = coefs.shape[1]
    knots = coefs.shape[2]
    share = rows // lax.axis_size("pred")
    start = lax.axis_index("pred") * share
    wl = jnp.broadcast_to(weight_table(H)[:, :, None], (4, H, L))
    padded = extended(coefs, (("tile", 1),), 2)
    along = banded_along(padded, ny)
    nrow = padded.shape[1]
    target_blk = lax.dynamic_slice_in_dim(target, start, share, 0)
    land_blk = lax.dynamic_slice_in_dim(land, start, share, 0).astype(jnp.float32)
    width = ny // CHUNKS
    fitted_parts, back_parts = [], []
    for c in range(CHUNKS):
        partial = fit_chunk(wl, covariates, along, c, width)
        total = allreduce_rows(partial, "pred")
        back_parts.append(back_chunk(wl, covariates, total, target, land, c, nrow))
        fitted_parts.append(lax.dynamic_slice_in_dim(total, start, share, 0))
    fitted = jnp.concatenate(fitted_parts, axis=1)
    residual = land_blk * (target_blk - fitted)
    back = jnp.concatenate(back_parts, axis=1)
    grad_pad = -(1.0 / H) * banded_data(back, knots)
    inner = grad_pad[:, 2 : count + 2]
    from_below = from_behind(grad_pad[:, count + 2 :], "tile", 1)
    from_above = from_behind(grad_pad[:, :2], "tile", -1)
    middle = jnp.zeros((inner.shape[0], count - 2, inner.shape[2]), jnp.float32)
    low_add = jnp.concatenate([from_below, middle], axis=1)
    high_add = jnp.concatenate([middle, from_above], axis=1)
    data = inner + low_add + high_add
    gradient = data + smoothing[:, None, None] * penalty(padded, count)
    new_first = 0.9 * first_moment + 0.1 * gradient
    new_second = 0.99 * second_moment + 0.01 * gradient * gradient
    new_coefs = coefs - 0.1 * new_first / (jnp.sqrt(new_second) + 1e-08)
    return (fitted, residual, gradient, new_coefs, new_first, new_second)


def solution(mesh):
    in_specs = (
        P("pred", "tile", None),
        P("tile", None),
        P("tile", None),
        P("pred", "tile", None),
        P("pred", "tile", None),
        P("pred", "tile", None),
        P("pred"),
    )
    out_specs = (
        P(("tile", "pred"), None),
        P(("tile", "pred"), None),
        P("pred", "tile", None),
        P("pred", "tile", None),
        P("pred", "tile", None),
        P("pred", "tile", None),
    )
    return jax.shard_map(local, mesh=mesh, in_specs=in_specs, out_specs=out_specs, check_vma=False)
```

```python
import jax
import jax.numpy as jnp
from jax import lax
from jax.experimental import pallas as pl
from jax.experimental.pallas import tpu as pltpu
from jax.sharding import PartitionSpec as P

H = 16
TN = 512
L = 256
CHUNKS = 4
LEAD = 8


def extended(array, sides, width):
    for axis, dim in sides:
        peers, length = (lax.axis_size(axis), array.shape[dim])
        up = [(i, (i + 1) % peers) for i in range(peers - 1)]
        down = [(j, i) for i, j in up]
        last = lax.slice_in_dim(array, length - width, length, axis=dim)
        first = lax.slice_in_dim(array, 0, width, axis=dim)
        before = lax.ppermute(last, axis, up)
        after = lax.ppermute(first, axis, down)
        array = jnp.concatenate([before, array, after], axis=dim)
    return array


def from_behind(block, axis, distance):
    devices = range(lax.axis_size(axis))
    route = [(i - distance, i) for i in devices if i - distance in devices]
    return lax.ppermute(block, axis, route)


def weights_of(u):
    return [
        (1.0 - u) * (1.0 - u) * (1.0 - u) / 6.0,
        (3.0 * u * u * u - 6.0 * u * u + 4.0) / 6.0,
        (-3.0 * u * u * u + 3.0 * u * u + 3.0 * u + 1.0) / 6.0,
        u * u * u / 6.0,
    ]


def weight_table(spacing):
    u = (jnp.arange(spacing, dtype=jnp.float32) + 0.5) / spacing
    return jnp.stack(weights_of(u))


def block_basis(window):
    n = jnp.arange(window, dtype=jnp.int32)[:, None]
    j = jnp.arange(TN, dtype=jnp.int32)[None, :]
    u = ((j % H).astype(jnp.float32) + 0.5) / H
    values = weights_of(u)
    offset = n - LEAD + 1 - j // H
    basis = jnp.zeros((window, TN), jnp.float32)
    for dd in range(4):
        basis = jnp.where(offset == dd, values[dd], basis)
    return basis


def banded_along(padded, ny):
    knots = padded.shape[-1]
    per_block = TN // H
    window = 4 * per_block
    blocks = ny // TN
    right = per_block * (blocks - 1) + window - knots - LEAD
    cpad = jnp.pad(padded, ((0, 0), (0, 0), (LEAD, right)))
    cwin = jnp.stack([cpad[..., per_block * b : per_block * b + window] for b in range(blocks)], axis=1)
    return jnp.einsum("pbkn,nj->pbkj", cwin, block_basis(window), precision=lax.Precision.HIGH)


def banded_data(back4, knots):
    npred, blocks, nrow, _ = back4.shape
    per_block = TN // H
    window = 4 * per_block
    dwin = jnp.einsum("pbkj,nj->pkbn", back4, block_basis(window), precision=lax.Precision.HIGH)
    total = None
    for a in range(4):
        part = dwin[..., a * per_block : (a + 1) * per_block]
        part = jnp.pad(part, ((0, 0), (0, 0), (a, 3 - a), (0, 0)))
        total = part if total is None else total + part
    total = total.reshape(npred, nrow, (blocks + 3) * per_block)
    return total[..., LEAD : LEAD + knots]


def reduce_steps(x, axis):
    n = lax.axis_size(axis)
    idx = lax.axis_index(axis)
    bits = []
    bit = 1
    while bit < n:
        bits.append(bit)
        bit *= 2
    steps = []
    for bit in bits:
        def halve(cur, bit=bit):
            half = cur.shape[0] // 2
            mine = (idx // bit) % 2
            pair = cur.reshape((2, half) + cur.shape[1:])
            keep = lax.dynamic_index_in_dim(pair, mine, 0, keepdims=False)
            send = lax.dynamic_index_in_dim(pair, 1 - mine, 0, keepdims=False)
            return send, lambda recv: keep + recv
        steps.append((bit, halve))
    for bit in reversed(bits):
        def double(cur, bit=bit):
            mine = (idx // bit) % 2
            def finish(other):
                first = jnp.where(mine == 0, cur, other)
                second = jnp.where(mine == 0, other, cur)
                return jnp.concatenate([first, second], axis=0)
            return cur, finish
        steps.append((bit, double))
    return [(bit, fn, [(i, i ^ bit) for i in range(n)]) for bit, fn in steps]


def fit_kernel(w_ref, cov_ref, a_ref, o_ref):
    npred = cov_ref.shape[0]
    nint = cov_ref.shape[1] // H
    for s in range(TN // L):
        cols = pl.ds(s * L, L)
        w = [w_ref[d] for d in range(4)]
        for m in range(nint):
            rows = pl.ds(m * H, H)

            def body(p, acc):
                surf = w[0] * a_ref[p, 0, pl.ds(m + 1, 1), cols]
                for d in range(1, 4):
                    surf = surf + w[d] * a_ref[p, 0, pl.ds(m + 1 + d, 1), cols]
                return acc + cov_ref[p, rows, cols].astype(jnp.float32) * surf

            acc = lax.fori_loop(0, npred, body, jnp.zeros((H, L), jnp.float32), unroll=True)
            o_ref[rows, cols] = acc


def back_kernel(w_ref, cov_ref, t_ref, y_ref, g_ref, o_ref, rw_ref):
    npred = cov_ref.shape[0]
    nint = cov_ref.shape[1] // H
    for s in range(TN // L):
        cols = pl.ds(s * L, L)
        for m in range(nint):
            rows = pl.ds(m * H, H)
            resid = g_ref[rows, cols].astype(jnp.float32) * (y_ref[rows, cols] - t_ref[rows, cols])
            for d in range(4):
                rw_ref[d, rows, :] = w_ref[d] * resid

        def body(p, carry):
            o_ref[p, 0, pl.ds(0, 1), cols] = jnp.zeros((1, L), jnp.float32)
            accs = {}
            for m in range(nint):
                c = cov_ref[p, pl.ds(m * H, H), cols].astype(jnp.float32)
                for d in range(4):
                    prod = c * rw_ref[d, pl.ds(m * H, H), :]
                    half = prod[0:8] + prod[8:16]
                    r = m + 1 + d
                    accs[r] = half if r not in accs else accs[r] + half
                done = m + 1
                o_ref[p, 0, pl.ds(done, 1), cols] = jnp.sum(accs.pop(done), axis=0, keepdims=True)
            for r in sorted(accs):
                o_ref[p, 0, pl.ds(r, 1), cols] = jnp.sum(accs[r], axis=0, keepdims=True)
            return carry

        lax.fori_loop(0, npred, body, 0)


def fit_chunk(wl, cov, along, chunk, width):
    npred, rows, _ = cov.shape
    nrow = along.shape[2]
    off = chunk * (width // TN)
    return pl.pallas_call(
        fit_kernel,
        grid=(width // TN,),
        in_specs=[
            pl.BlockSpec((4, H, L), lambda j: (0, 0, 0)),
            pl.BlockSpec((npred, rows, TN), lambda j: (0, 0, j + off)),
            pl.BlockSpec((npred, 1, nrow, TN), lambda j: (0, j + off, 0, 0)),
        ],
        out_specs=pl.BlockSpec((rows, TN), lambda j: (0, j)),
        out_shape=jax.ShapeDtypeStruct((rows, width), jnp.float32),
        compiler_params=pltpu.CompilerParams(dimension_semantics=("arbitrary",)),
        cost_estimate=pl.CostEstimate(
            flops=10 * npred * rows * width,
            transcendentals=0,
            bytes_accessed=2 * npred * rows * width + 4 * npred * nrow * width + 4 * rows * width,
        ),
    )(wl, cov, along)


def back_chunk(wl, cov, total, target, land, chunk, nrow):
    npred, rows, _ = cov.shape
    width = total.shape[1]
    off = chunk * (width // TN)
    return pl.pallas_call(
        back_kernel,
        grid=(width // TN,),
        in_specs=[
            pl.BlockSpec((4, H, L), lambda j: (0, 0, 0)),
            pl.BlockSpec((npred, rows, TN), lambda j: (0, 0, j + off)),
            pl.BlockSpec((rows, TN), lambda j: (0, j)),
            pl.BlockSpec((rows, TN), lambda j: (0, j + off)),
            pl.BlockSpec((rows, TN), lambda j: (0, j + off)),
        ],
        out_specs=pl.BlockSpec((npred, 1, nrow, TN), lambda j: (0, j, 0, 0)),
        out_shape=jax.ShapeDtypeStruct((npred, width // TN, nrow, TN), jnp.float32),
        scratch_shapes=[pltpu.VMEM((4, rows, L), jnp.float32)],
        compiler_params=pltpu.CompilerParams(dimension_semantics=("arbitrary",)),
        cost_estimate=pl.CostEstimate(
            flops=10 * npred * rows * width,
            transcendentals=0,
            bytes_accessed=2 * npred * rows * width + 12 * rows * width + 4 * npred * nrow * width,
        ),
    )(wl, cov, total, target, land)


def penalty(padded, count):
    stencil = [1.0, -4.0, 6.0, -4.0, 1.0]
    along_rows = None
    for ii in range(5):
        term = stencil[ii] * padded[..., ii : ii + count, :]
        along_rows = term if along_rows is None else along_rows + term
    centre = padded[..., 2 : count + 2, :]
    width = centre.shape[-1]
    wide = jnp.pad(centre, [(0, 0)] * (centre.ndim - 1) + [(2, 2)])
    for ii in range(5):
        along_rows = along_rows + stencil[ii] * wide[..., ii : ii + width]
    return along_rows


def local(covariates, target, land, coefs, first_moment, second_moment, smoothing):
    npred, rows, ny = covariates.shape
    count = coefs.shape[1]
    knots = coefs.shape[2]
    share = rows // lax.axis_size("pred")
    start = lax.axis_index("pred") * share
    wl = jnp.broadcast_to(weight_table(H)[:, :, None], (4, H, L))
    padded = extended(coefs, (("tile", 1),), 2)
    along = banded_along(padded, ny)
    nrow = padded.shape[1]
    target_blk = lax.dynamic_slice_in_dim(target, start, share, 0)
    land_blk = lax.dynamic_slice_in_dim(land, start, share, 0).astype(jnp.float32)
    width = ny // CHUNKS
    steps = reduce_steps(jnp.zeros((rows, width), jnp.float32), "pred")
    nsteps = len(steps)
    state = [None] * CHUNKS
    fitted_parts = [None] * CHUNKS
    back_parts = [None] * CHUNKS
    state[0] = fit_chunk(wl, covariates, along, 0, width)
    for s in range(1, CHUNKS + nsteps + 1):
        pending = []
        for c in range(CHUNKS):
            k = s - c - 1
            if 0 <= k < nsteps:
                _, fn, pairs = steps[k]
                send, finish = fn(state[c])
                pending.append((c, finish, lax.ppermute(send, "pred", pairs)))
        filler = None
        if s < CHUNKS:
            filler = ("fit", s)
        elif 0 <= s - nsteps - 1 < CHUNKS:
            filler = ("back", s - nsteps - 1)
        recvs = [r for _, _, r in pending]
        if filler is not None:
            kind, c = filler
            if kind == "fit":
                out = fit_chunk(wl, covariates, along, c, width)
            else:
                out = back_chunk(wl, covariates, state[c], target, land, c, nrow)
            recvs, out = lax.optimization_barrier((recvs, out))
            if kind == "fit":
                state[c] = out
            else:
                back_parts[c] = out
        for (c, finish, _), r in zip(pending, recvs):
            state[c] = finish(r)
    for c in range(CHUNKS):
        if back_parts[c] is None:
            back_parts[c] = back_chunk(wl, covariates, state[c], target, land, c, nrow)
        fitted_parts[c] = lax.dynamic_slice_in_dim(state[c], start, share, 0)
    fitted = jnp.concatenate(fitted_parts, axis=1)
    residual = land_blk * (target_blk - fitted)
    back = jnp.concatenate(back_parts, axis=1)
    grad_pad = -(1.0 / H) * banded_data(back, knots)
    inner = grad_pad[:, 2 : count + 2]
    from_below = from_behind(grad_pad[:, count + 2 :], "tile", 1)
    from_above = from_behind(grad_pad[:, :2], "tile", -1)
    middle = jnp.zeros((inner.shape[0], count - 2, inner.shape[2]), jnp.float32)
    low_add = jnp.concatenate([from_below, middle], axis=1)
    high_add = jnp.concatenate([middle, from_above], axis=1)
    data = inner + low_add + high_add
    gradient = data + smoothing[:, None, None] * penalty(padded, count)
    new_first = 0.9 * first_moment + 0.1 * gradient
    new_second = 0.99 * second_moment + 0.01 * gradient * gradient
    new_coefs = coefs - 0.1 * new_first / (jnp.sqrt(new_second) + 1e-08)
    return (fitted, residual, gradient, new_coefs, new_first, new_second)


def solution(mesh):
    in_specs = (
        P("pred", "tile", None),
        P("tile", None),
        P("tile", None),
        P("pred", "tile", None),
        P("pred", "tile", None),
        P("pred", "tile", None),
        P("pred"),
    )
    out_specs = (
        P(("tile", "pred"), None),
        P(("tile", "pred"), None),
        P("pred", "tile", None),
        P("pred", "tile", None),
        P("pred", "tile", None),
        P("pred", "tile", None),
    )
    return jax.shard_map(local, mesh=mesh, in_specs=in_specs, out_specs=out_specs, check_vma=False)
```

```python
import jax
import jax.numpy as jnp
from jax import lax
from jax.experimental import pallas as pl
from jax.experimental.pallas import tpu as pltpu
from jax.sharding import PartitionSpec as P

H = 16
TN = 512
L = 256
CHUNKS = 8
LEAD = 8


def extended(array, sides, width):
    for axis, dim in sides:
        peers, length = (lax.axis_size(axis), array.shape[dim])
        up = [(i, (i + 1) % peers) for i in range(peers - 1)]
        down = [(j, i) for i, j in up]
        last = lax.slice_in_dim(array, length - width, length, axis=dim)
        first = lax.slice_in_dim(array, 0, width, axis=dim)
        before = lax.ppermute(last, axis, up)
        after = lax.ppermute(first, axis, down)
        array = jnp.concatenate([before, array, after], axis=dim)
    return array


def from_behind(block, axis, distance):
    devices = range(lax.axis_size(axis))
    route = [(i - distance, i) for i in devices if i - distance in devices]
    return lax.ppermute(block, axis, route)


def weights_of(u):
    return [
        (1.0 - u) * (1.0 - u) * (1.0 - u) / 6.0,
        (3.0 * u * u * u - 6.0 * u * u + 4.0) / 6.0,
        (-3.0 * u * u * u + 3.0 * u * u + 3.0 * u + 1.0) / 6.0,
        u * u * u / 6.0,
    ]


def weight_table(spacing):
    u = (jnp.arange(spacing, dtype=jnp.float32) + 0.5) / spacing
    return jnp.stack(weights_of(u))


def block_basis(window):
    n = jnp.arange(window, dtype=jnp.int32)[:, None]
    j = jnp.arange(TN, dtype=jnp.int32)[None, :]
    u = ((j % H).astype(jnp.float32) + 0.5) / H
    values = weights_of(u)
    offset = n - LEAD + 1 - j // H
    basis = jnp.zeros((window, TN), jnp.float32)
    for dd in range(4):
        basis = jnp.where(offset == dd, values[dd], basis)
    return basis


def banded_along(padded, ny):
    knots = padded.shape[-1]
    per_block = TN // H
    window = 4 * per_block
    blocks = ny // TN
    right = per_block * (blocks - 1) + window - knots - LEAD
    cpad = jnp.pad(padded, ((0, 0), (0, 0), (LEAD, right)))
    cwin = jnp.stack([cpad[..., per_block * b : per_block * b + window] for b in range(blocks)], axis=1)
    return jnp.einsum("pbkn,nj->pbkj", cwin, block_basis(window), precision=lax.Precision.HIGH)


def banded_data(back4, knots):
    npred, blocks, nrow, _ = back4.shape
    per_block = TN // H
    window = 4 * per_block
    dwin = jnp.einsum("pbkj,nj->pbkn", back4, block_basis(window), precision=lax.Precision.HIGH)
    dwin = jnp.transpose(dwin, (0, 2, 1, 3))
    total = None
    for a in range(4):
        part = dwin[..., a * per_block : (a + 1) * per_block]
        part = jnp.pad(part, ((0, 0), (0, 0), (a, 3 - a), (0, 0)))
        total = part if total is None else total + part
    total = total.reshape(npred, nrow, (blocks + 3) * per_block)
    return total[..., LEAD : LEAD + knots]


def reduce_steps(x, axis):
    n = lax.axis_size(axis)
    idx = lax.axis_index(axis)
    bits = []
    bit = 1
    while bit < n:
        bits.append(bit)
        bit *= 2
    steps = []
    for bit in bits:
        def halve(cur, bit=bit):
            half = cur.shape[0] // 2
            mine = (idx // bit) % 2
            pair = cur.reshape((2, half) + cur.shape[1:])
            keep = lax.dynamic_index_in_dim(pair, mine, 0, keepdims=False)
            send = lax.dynamic_index_in_dim(pair, 1 - mine, 0, keepdims=False)
            return send, lambda recv: keep + recv
        steps.append((bit, halve))
    for bit in reversed(bits):
        def double(cur, bit=bit):
            mine = (idx // bit) % 2
            def finish(other):
                first = jnp.where(mine == 0, cur, other)
                second = jnp.where(mine == 0, other, cur)
                return jnp.concatenate([first, second], axis=0)
            return cur, finish
        steps.append((bit, double))
    return [(bit, fn, [(i, i ^ bit) for i in range(n)]) for bit, fn in steps]


def fit_kernel(w_ref, cov_ref, a_ref, o_ref):
    npred = cov_ref.shape[0]
    nint = cov_ref.shape[1] // H
    for s in range(TN // L):
        cols = pl.ds(s * L, L)
        w = [w_ref[d] for d in range(4)]
        for m in range(nint):
            rows = pl.ds(m * H, H)

            def body(p, acc):
                surf = w[0] * a_ref[p, 0, pl.ds(m + 1, 1), cols]
                for d in range(1, 4):
                    surf = surf + w[d] * a_ref[p, 0, pl.ds(m + 1 + d, 1), cols]
                return acc + cov_ref[p, rows, cols].astype(jnp.float32) * surf

            acc = lax.fori_loop(0, npred, body, jnp.zeros((H, L), jnp.float32), unroll=True)
            o_ref[rows, cols] = acc


def back_kernel(w_ref, cov_ref, t_ref, y_ref, g_ref, o_ref, rw_ref):
    npred = cov_ref.shape[0]
    nint = cov_ref.shape[1] // H
    for s in range(TN // L):
        cols = pl.ds(s * L, L)
        for m in range(nint):
            rows = pl.ds(m * H, H)
            resid = g_ref[rows, cols].astype(jnp.float32) * (y_ref[rows, cols] - t_ref[rows, cols])
            for d in range(4):
                rw_ref[d, rows, :] = w_ref[d] * resid

        def body(p, carry):
            o_ref[p, 0, pl.ds(0, 1), cols] = jnp.zeros((1, L), jnp.float32)
            accs = {}
            for m in range(nint):
                c = cov_ref[p, pl.ds(m * H, H), cols].astype(jnp.float32)
                for d in range(4):
                    prod = c * rw_ref[d, pl.ds(m * H, H), :]
                    r = m + 1 + d
                    accs[r] = prod if r not in accs else accs[r] + prod
                done = m + 1
                o_ref[p, 0, pl.ds(done, 1), cols] = jnp.sum(accs.pop(done), axis=0, keepdims=True)
            for r in sorted(accs):
                o_ref[p, 0, pl.ds(r, 1), cols] = jnp.sum(accs[r], axis=0, keepdims=True)
            return carry

        lax.fori_loop(0, npred, body, 0)


def fit_chunk(wl, cov, along, chunk, width):
    npred, rows, _ = cov.shape
    nrow = along.shape[2]
    off = chunk * (width // TN)
    return pl.pallas_call(
        fit_kernel,
        grid=(width // TN,),
        in_specs=[
            pl.BlockSpec((4, H, L), lambda j: (0, 0, 0)),
            pl.BlockSpec((npred, rows, TN), lambda j: (0, 0, j + off)),
            pl.BlockSpec((npred, 1, nrow, TN), lambda j: (0, j + off, 0, 0)),
        ],
        out_specs=pl.BlockSpec((rows, TN), lambda j: (0, j)),
        out_shape=jax.ShapeDtypeStruct((rows, width), jnp.float32),
        compiler_params=pltpu.CompilerParams(dimension_semantics=("arbitrary",)),
        cost_estimate=pl.CostEstimate(
            flops=10 * npred * rows * width,
            transcendentals=0,
            bytes_accessed=2 * npred * rows * width + 4 * npred * nrow * width + 4 * rows * width,
        ),
    )(wl, cov, along)


def back_chunk(wl, cov, total, target, land, chunk, nrow):
    npred, rows, _ = cov.shape
    width = total.shape[1]
    off = chunk * (width // TN)
    return pl.pallas_call(
        back_kernel,
        grid=(width // TN,),
        in_specs=[
            pl.BlockSpec((4, H, L), lambda j: (0, 0, 0)),
            pl.BlockSpec((npred, rows, TN), lambda j: (0, 0, j + off)),
            pl.BlockSpec((rows, TN), lambda j: (0, j)),
            pl.BlockSpec((rows, TN), lambda j: (0, j + off)),
            pl.BlockSpec((rows, TN), lambda j: (0, j + off)),
        ],
        out_specs=pl.BlockSpec((npred, 1, nrow, TN), lambda j: (0, j, 0, 0)),
        out_shape=jax.ShapeDtypeStruct((npred, width // TN, nrow, TN), jnp.float32),
        scratch_shapes=[pltpu.VMEM((4, rows, L), jnp.float32)],
        compiler_params=pltpu.CompilerParams(dimension_semantics=("arbitrary",)),
        cost_estimate=pl.CostEstimate(
            flops=10 * npred * rows * width,
            transcendentals=0,
            bytes_accessed=2 * npred * rows * width + 12 * rows * width + 4 * npred * nrow * width,
        ),
    )(wl, cov, total, target, land)


def penalty(padded, count):
    stencil = [1.0, -4.0, 6.0, -4.0, 1.0]
    along_rows = None
    for ii in range(5):
        term = stencil[ii] * padded[..., ii : ii + count, :]
        along_rows = term if along_rows is None else along_rows + term
    centre = padded[..., 2 : count + 2, :]
    width = centre.shape[-1]
    wide = jnp.pad(centre, [(0, 0)] * (centre.ndim - 1) + [(2, 2)])
    for ii in range(5):
        along_rows = along_rows + stencil[ii] * wide[..., ii : ii + width]
    return along_rows


def local(covariates, target, land, coefs, first_moment, second_moment, smoothing):
    npred, rows, ny = covariates.shape
    count = coefs.shape[1]
    knots = coefs.shape[2]
    share = rows // lax.axis_size("pred")
    start = lax.axis_index("pred") * share
    wl = jnp.broadcast_to(weight_table(H)[:, :, None], (4, H, L))
    padded = extended(coefs, (("tile", 1),), 2)
    along = banded_along(padded, ny)
    nrow = padded.shape[1]
    target_blk = lax.dynamic_slice_in_dim(target, start, share, 0)
    land_blk = lax.dynamic_slice_in_dim(land, start, share, 0).astype(jnp.float32)
    width = ny // CHUNKS
    steps = reduce_steps(jnp.zeros((rows, width), jnp.float32), "pred")
    nsteps = len(steps)
    state = [None] * CHUNKS
    fitted_parts = [None] * CHUNKS
    back_parts = [None] * CHUNKS
    state[0] = fit_chunk(wl, covariates, along, 0, width)
    next_back = 0
    for s in range(1, CHUNKS + nsteps + 1):
        pending = []
        for c in range(CHUNKS):
            k = s - c - 1
            if 0 <= k < nsteps:
                _, fn, pairs = steps[k]
                send, finish = fn(state[c])
                pending.append((c, finish, lax.ppermute(send, "pred", pairs)))
        outs = []
        if s < CHUNKS:
            outs.append(("fit", s, fit_chunk(wl, covariates, along, s, width)))
        if next_back < CHUNKS and next_back + nsteps + 1 <= s:
            c = next_back
            outs.append(("back", c, back_chunk(wl, covariates, state[c], target, land, c, nrow)))
            next_back += 1
        recvs = [r for _, _, r in pending]
        if outs:
            recvs, vals = lax.optimization_barrier((recvs, [v for _, _, v in outs]))
            for (kind, c, _), v in zip(outs, vals):
                if kind == "fit":
                    state[c] = v
                else:
                    back_parts[c] = v
        for (c, finish, _), r in zip(pending, recvs):
            state[c] = finish(r)
    for c in range(CHUNKS):
        if back_parts[c] is None:
            back_parts[c] = back_chunk(wl, covariates, state[c], target, land, c, nrow)
        fitted_parts[c] = lax.dynamic_slice_in_dim(state[c], start, share, 0)
    fitted = jnp.concatenate(fitted_parts, axis=1)
    residual = land_blk * (target_blk - fitted)
    back = jnp.concatenate(back_parts, axis=1)
    grad_pad = -(1.0 / H) * banded_data(back, knots)
    inner = grad_pad[:, 2 : count + 2]
    from_below = from_behind(grad_pad[:, count + 2 :], "tile", 1)
    from_above = from_behind(grad_pad[:, :2], "tile", -1)
    middle = jnp.zeros((inner.shape[0], count - 2, inner.shape[2]), jnp.float32)
    low_add = jnp.concatenate([from_below, middle], axis=1)
    high_add = jnp.concatenate([middle, from_above], axis=1)
    data = inner + low_add + high_add
    gradient = data + smoothing[:, None, None] * penalty(padded, count)
    new_first = 0.9 * first_moment + 0.1 * gradient
    new_second = 0.99 * second_moment + 0.01 * gradient * gradient
    new_coefs = coefs - 0.1 * new_first / (jnp.sqrt(new_second) + 1e-08)
    return (fitted, residual, gradient, new_coefs, new_first, new_second)


def solution(mesh):
    in_specs = (
        P("pred", "tile", None),
        P("tile", None),
        P("tile", None),
        P("pred", "tile", None),
        P("pred", "tile", None),
        P("pred", "tile", None),
        P("pred"),
    )
    out_specs = (
        P(("tile", "pred"), None),
        P(("tile", "pred"), None),
        P("pred", "tile", None),
        P("pred", "tile", None),
        P("pred", "tile", None),
        P("pred", "tile", None),
    )
    return jax.shard_map(local, mesh=mesh, in_specs=in_specs, out_specs=out_specs, check_vma=False)
```

```python
import jax
import jax.numpy as jnp
from jax import lax
from jax.experimental import pallas as pl
from jax.experimental.pallas import tpu as pltpu
from jax.sharding import PartitionSpec as P

H = 16
TN = 512
L = 256
CHUNKS = 4
LEAD = 8


def extended(array, sides, width):
    for axis, dim in sides:
        peers, length = (lax.axis_size(axis), array.shape[dim])
        up = [(i, (i + 1) % peers) for i in range(peers - 1)]
        down = [(j, i) for i, j in up]
        last = lax.slice_in_dim(array, length - width, length, axis=dim)
        first = lax.slice_in_dim(array, 0, width, axis=dim)
        before = lax.ppermute(last, axis, up)
        after = lax.ppermute(first, axis, down)
        array = jnp.concatenate([before, array, after], axis=dim)
    return array


def from_behind(block, axis, distance):
    devices = range(lax.axis_size(axis))
    route = [(i - distance, i) for i in devices if i - distance in devices]
    return lax.ppermute(block, axis, route)


def weights_of(u):
    return [
        (1.0 - u) * (1.0 - u) * (1.0 - u) / 6.0,
        (3.0 * u * u * u - 6.0 * u * u + 4.0) / 6.0,
        (-3.0 * u * u * u + 3.0 * u * u + 3.0 * u + 1.0) / 6.0,
        u * u * u / 6.0,
    ]


def weight_table(spacing):
    u = (jnp.arange(spacing, dtype=jnp.float32) + 0.5) / spacing
    return jnp.stack(weights_of(u))


def block_basis(window):
    n = jnp.arange(window, dtype=jnp.int32)[:, None]
    j = jnp.arange(TN, dtype=jnp.int32)[None, :]
    u = ((j % H).astype(jnp.float32) + 0.5) / H
    values = weights_of(u)
    offset = n - LEAD + 1 - j // H
    basis = jnp.zeros((window, TN), jnp.float32)
    for dd in range(4):
        basis = jnp.where(offset == dd, values[dd], basis)
    return basis


def banded_along(padded, ny):
    knots = padded.shape[-1]
    per_block = TN // H
    window = 4 * per_block
    blocks = ny // TN
    right = per_block * (blocks - 1) + window - knots - LEAD
    cpad = jnp.pad(padded, ((0, 0), (0, 0), (LEAD, right)))
    cwin = jnp.stack([cpad[..., per_block * b : per_block * b + window] for b in range(blocks)], axis=1)
    return jnp.einsum("pbkn,nj->pbkj", cwin, block_basis(window), precision=lax.Precision.HIGH)


def banded_data(back4, knots):
    npred, blocks, nrow, _ = back4.shape
    per_block = TN // H
    window = 4 * per_block
    dwin = jnp.einsum("pbkj,nj->pkbn", back4, block_basis(window), precision=lax.Precision.HIGH)
    total = None
    for a in range(4):
        part = dwin[..., a * per_block : (a + 1) * per_block]
        part = jnp.pad(part, ((0, 0), (0, 0), (a, 3 - a), (0, 0)))
        total = part if total is None else total + part
    total = total.reshape(npred, nrow, (blocks + 3) * per_block)
    return total[..., LEAD : LEAD + knots]


def reduce_steps(x, axis):
    n = lax.axis_size(axis)
    idx = lax.axis_index(axis)
    bits = []
    bit = 1
    while bit < n:
        bits.append(bit)
        bit *= 2
    steps = []
    for bit in bits[:-1]:
        def halve(cur, bit=bit):
            half = cur.shape[0] // 2
            mine = (idx // bit) % 2
            pair = cur.reshape((2, half) + cur.shape[1:])
            keep = lax.dynamic_index_in_dim(pair, mine, 0, keepdims=False)
            send = lax.dynamic_index_in_dim(pair, 1 - mine, 0, keepdims=False)
            return send, lambda recv: keep + recv
        steps.append((bit, halve))
    for bit in bits[-1:]:
        def swap(cur):
            return cur, lambda recv: cur + recv
        steps.append((bit, swap))
    for bit in reversed(bits[:-1]):
        def double(cur, bit=bit):
            mine = (idx // bit) % 2
            def finish(other):
                first = jnp.where(mine == 0, cur, other)
                second = jnp.where(mine == 0, other, cur)
                return jnp.concatenate([first, second], axis=0)
            return cur, finish
        steps.append((bit, double))
    return [(bit, fn, [(i, i ^ bit) for i in range(n)]) for bit, fn in steps]


def fit_kernel(w_ref, cov_ref, a_ref, o_ref):
    npred = cov_ref.shape[0]
    nint = cov_ref.shape[1] // H
    for s in range(TN // L):
        cols = pl.ds(s * L, L)
        w = [w_ref[d] for d in range(4)]
        for m in range(nint):
            rows = pl.ds(m * H, H)

            def body(p, acc):
                surf = w[0] * a_ref[p, 0, pl.ds(m + 1, 1), cols]
                for d in range(1, 4):
                    surf = surf + w[d] * a_ref[p, 0, pl.ds(m + 1 + d, 1), cols]
                return acc + cov_ref[p, rows, cols].astype(jnp.float32) * surf

            acc = lax.fori_loop(0, npred, body, jnp.zeros((H, L), jnp.float32), unroll=True)
            o_ref[rows, cols] = acc


def back_kernel(w_ref, cov_ref, t_ref, y_ref, g_ref, o_ref, rw_ref):
    npred = cov_ref.shape[0]
    nint = cov_ref.shape[1] // H
    for s in range(TN // L):
        cols = pl.ds(s * L, L)
        for m in range(nint):
            rows = pl.ds(m * H, H)
            resid = g_ref[rows, cols].astype(jnp.float32) * (y_ref[rows, cols] - t_ref[rows, cols])
            for d in range(4):
                rw_ref[d, rows, :] = w_ref[d] * resid

        def body(p, carry):
            o_ref[p, 0, pl.ds(0, 1), cols] = jnp.zeros((1, L), jnp.float32)
            accs = {}
            for m in range(nint):
                c = cov_ref[p, pl.ds(m * H, H), cols].astype(jnp.float32)
                for d in range(4):
                    prod = c * rw_ref[d, pl.ds(m * H, H), :]
                    half = prod[0:8] + prod[8:16]
                    r = m + 1 + d
                    accs[r] = half if r not in accs else accs[r] + half
                done = m + 1
                o_ref[p, 0, pl.ds(done, 1), cols] = jnp.sum(accs.pop(done), axis=0, keepdims=True)
            for r in sorted(accs):
                o_ref[p, 0, pl.ds(r, 1), cols] = jnp.sum(accs[r], axis=0, keepdims=True)
            return carry

        lax.fori_loop(0, npred, body, 0)


def fit_chunk(wl, cov, along, chunk, width):
    npred, rows, _ = cov.shape
    nrow = along.shape[2]
    off = chunk * (width // TN)
    return pl.pallas_call(
        fit_kernel,
        grid=(width // TN,),
        in_specs=[
            pl.BlockSpec((4, H, L), lambda j: (0, 0, 0)),
            pl.BlockSpec((npred, rows, TN), lambda j: (0, 0, j + off)),
            pl.BlockSpec((npred, 1, nrow, TN), lambda j: (0, j + off, 0, 0)),
        ],
        out_specs=pl.BlockSpec((rows, TN), lambda j: (0, j)),
        out_shape=jax.ShapeDtypeStruct((rows, width), jnp.float32),
        compiler_params=pltpu.CompilerParams(dimension_semantics=("arbitrary",)),
        cost_estimate=pl.CostEstimate(
            flops=10 * npred * rows * width,
            transcendentals=0,
            bytes_accessed=2 * npred * rows * width + 4 * npred * nrow * width + 4 * rows * width,
        ),
    )(wl, cov, along)


def back_chunk(wl, cov, total, target, land, chunk, nrow):
    npred, rows, _ = cov.shape
    width = total.shape[1]
    off = chunk * (width // TN)
    return pl.pallas_call(
        back_kernel,
        grid=(width // TN,),
        in_specs=[
            pl.BlockSpec((4, H, L), lambda j: (0, 0, 0)),
            pl.BlockSpec((npred, rows, TN), lambda j: (0, 0, j + off)),
            pl.BlockSpec((rows, TN), lambda j: (0, j)),
            pl.BlockSpec((rows, TN), lambda j: (0, j + off)),
            pl.BlockSpec((rows, TN), lambda j: (0, j + off)),
        ],
        out_specs=pl.BlockSpec((npred, 1, nrow, TN), lambda j: (0, j, 0, 0)),
        out_shape=jax.ShapeDtypeStruct((npred, width // TN, nrow, TN), jnp.float32),
        scratch_shapes=[pltpu.VMEM((4, rows, L), jnp.float32)],
        compiler_params=pltpu.CompilerParams(dimension_semantics=("arbitrary",)),
        cost_estimate=pl.CostEstimate(
            flops=10 * npred * rows * width,
            transcendentals=0,
            bytes_accessed=2 * npred * rows * width + 12 * rows * width + 4 * npred * nrow * width,
        ),
    )(wl, cov, total, target, land)


def penalty(padded, count):
    stencil = [1.0, -4.0, 6.0, -4.0, 1.0]
    along_rows = None
    for ii in range(5):
        term = stencil[ii] * padded[..., ii : ii + count, :]
        along_rows = term if along_rows is None else along_rows + term
    centre = padded[..., 2 : count + 2, :]
    width = centre.shape[-1]
    wide = jnp.pad(centre, [(0, 0)] * (centre.ndim - 1) + [(2, 2)])
    for ii in range(5):
        along_rows = along_rows + stencil[ii] * wide[..., ii : ii + width]
    return along_rows


def local(covariates, target, land, coefs, first_moment, second_moment, smoothing):
    npred, rows, ny = covariates.shape
    count = coefs.shape[1]
    knots = coefs.shape[2]
    share = rows // lax.axis_size("pred")
    start = lax.axis_index("pred") * share
    wl = jnp.broadcast_to(weight_table(H)[:, :, None], (4, H, L))
    padded = extended(coefs, (("tile", 1),), 2)
    along = banded_along(padded, ny)
    nrow = padded.shape[1]
    target_blk = lax.dynamic_slice_in_dim(target, start, share, 0)
    land_blk = lax.dynamic_slice_in_dim(land, start, share, 0).astype(jnp.float32)
    width = ny // CHUNKS
    steps = reduce_steps(jnp.zeros((rows, width), jnp.float32), "pred")
    nsteps = len(steps)
    state = [None] * CHUNKS
    fitted_parts = [None] * CHUNKS
    back_parts = [None] * CHUNKS
    state[0] = fit_chunk(wl, covariates, along, 0, width)
    next_back = 0
    for s in range(1, CHUNKS + nsteps + 1):
        pending = []
        for c in range(CHUNKS):
            k = s - c - 1
            if 0 <= k < nsteps:
                _, fn, pairs = steps[k]
                send, finish = fn(state[c])
                pending.append((c, finish, lax.ppermute(send, "pred", pairs)))
        outs = []
        if s < CHUNKS:
            outs.append(("fit", s, fit_chunk(wl, covariates, along, s, width)))
        if next_back < CHUNKS and next_back + nsteps + 1 <= s:
            c = next_back
            outs.append(("back", c, back_chunk(wl, covariates, state[c], target, land, c, nrow)))
            next_back += 1
        recvs = [r for _, _, r in pending]
        if outs:
            recvs, vals = lax.optimization_barrier((recvs, [v for _, _, v in outs]))
            for (kind, c, _), v in zip(outs, vals):
                if kind == "fit":
                    state[c] = v
                else:
                    back_parts[c] = v
        for (c, finish, _), r in zip(pending, recvs):
            state[c] = finish(r)
    for c in range(CHUNKS):
        if back_parts[c] is None:
            back_parts[c] = back_chunk(wl, covariates, state[c], target, land, c, nrow)
        fitted_parts[c] = lax.dynamic_slice_in_dim(state[c], start, share, 0)
    fitted = jnp.concatenate(fitted_parts, axis=1)
    residual = land_blk * (target_blk - fitted)
    back = jnp.concatenate(back_parts, axis=1)
    grad_pad = -(1.0 / H) * banded_data(back, knots)
    inner = grad_pad[:, 2 : count + 2]
    from_below = from_behind(grad_pad[:, count + 2 :], "tile", 1)
    from_above = from_behind(grad_pad[:, :2], "tile", -1)
    middle = jnp.zeros((inner.shape[0], count - 2, inner.shape[2]), jnp.float32)
    low_add = jnp.concatenate([from_below, middle], axis=1)
    high_add = jnp.concatenate([middle, from_above], axis=1)
    data = inner + low_add + high_add
    gradient = data + smoothing[:, None, None] * penalty(padded, count)
    new_first = 0.9 * first_moment + 0.1 * gradient
    new_second = 0.99 * second_moment + 0.01 * gradient * gradient
    new_coefs = coefs - 0.1 * new_first / (jnp.sqrt(new_second) + 1e-08)
    return (fitted, residual, gradient, new_coefs, new_first, new_second)


def solution(mesh):
    in_specs = (
        P("pred", "tile", None),
        P("tile", None),
        P("tile", None),
        P("pred", "tile", None),
        P("pred", "tile", None),
        P("pred", "tile", None),
        P("pred"),
    )
    out_specs = (
        P(("tile", "pred"), None),
        P(("tile", "pred"), None),
        P("pred", "tile", None),
        P("pred", "tile", None),
        P("pred", "tile", None),
        P("pred", "tile", None),
    )
    return jax.shard_map(local, mesh=mesh, in_specs=in_specs, out_specs=out_specs, check_vma=False)
```

```python
import jax
import jax.numpy as jnp
from jax import lax
from jax.experimental import pallas as pl
from jax.experimental.pallas import tpu as pltpu
from jax.sharding import PartitionSpec as P

H = 16
TN = 512
L = 256
CHUNKS = 4
LEAD = 8


def extended(array, sides, width):
    for axis, dim in sides:
        peers, length = (lax.axis_size(axis), array.shape[dim])
        up = [(i, (i + 1) % peers) for i in range(peers - 1)]
        down = [(j, i) for i, j in up]
        last = lax.slice_in_dim(array, length - width, length, axis=dim)
        first = lax.slice_in_dim(array, 0, width, axis=dim)
        before = lax.ppermute(last, axis, up)
        after = lax.ppermute(first, axis, down)
        array = jnp.concatenate([before, array, after], axis=dim)
    return array


def from_behind(block, axis, distance):
    devices = range(lax.axis_size(axis))
    route = [(i - distance, i) for i in devices if i - distance in devices]
    return lax.ppermute(block, axis, route)


def weights_of(u):
    return [
        (1.0 - u) * (1.0 - u) * (1.0 - u) / 6.0,
        (3.0 * u * u * u - 6.0 * u * u + 4.0) / 6.0,
        (-3.0 * u * u * u + 3.0 * u * u + 3.0 * u + 1.0) / 6.0,
        u * u * u / 6.0,
    ]


def weight_table(spacing):
    u = (jnp.arange(spacing, dtype=jnp.float32) + 0.5) / spacing
    return jnp.stack(weights_of(u))


def block_basis(window):
    n = jnp.arange(window, dtype=jnp.int32)[:, None]
    j = jnp.arange(TN, dtype=jnp.int32)[None, :]
    u = ((j % H).astype(jnp.float32) + 0.5) / H
    values = weights_of(u)
    offset = n - LEAD + 1 - j // H
    basis = jnp.zeros((window, TN), jnp.float32)
    for dd in range(4):
        basis = jnp.where(offset == dd, values[dd], basis)
    return basis


def banded_along(padded, ny):
    knots = padded.shape[-1]
    per_block = TN // H
    window = 4 * per_block
    blocks = ny // TN
    right = per_block * (blocks - 1) + window - knots - LEAD
    cpad = jnp.pad(padded, ((0, 0), (0, 0), (LEAD, right)))
    cwin = jnp.stack([cpad[..., per_block * b : per_block * b + window] for b in range(blocks)], axis=1)
    return jnp.einsum("pbkn,nj->pbkj", cwin, block_basis(window), precision=lax.Precision.HIGH)


def banded_data(back4, knots):
    npred, blocks, nrow, _ = back4.shape
    per_block = TN // H
    window = 4 * per_block
    dwin = jnp.einsum("pbkj,nj->pkbn", back4, block_basis(window), precision=lax.Precision.HIGH)
    total = None
    for a in range(4):
        part = dwin[..., a * per_block : (a + 1) * per_block]
        part = jnp.pad(part, ((0, 0), (0, 0), (a, 3 - a), (0, 0)))
        total = part if total is None else total + part
    total = total.reshape(npred, nrow, (blocks + 3) * per_block)
    return total[..., LEAD : LEAD + knots]


def reduce_steps(x, axis):
    n = lax.axis_size(axis)
    idx = lax.axis_index(axis)
    bits = []
    bit = 1
    while bit < n:
        bits.append(bit)
        bit *= 2
    steps = []
    for bit in bits[:-1]:
        def halve(cur, bit=bit):
            half = cur.shape[0] // 2
            mine = (idx // bit) % 2
            pair = cur.reshape((2, half) + cur.shape[1:])
            keep = lax.dynamic_index_in_dim(pair, mine, 0, keepdims=False)
            send = lax.dynamic_index_in_dim(pair, 1 - mine, 0, keepdims=False)
            return send, lambda recv: keep + recv
        steps.append((bit, halve))
    for bit in bits[-1:]:
        def swap(cur):
            return cur, lambda recv: cur + recv
        steps.append((bit, swap))
    for bit in reversed(bits[:-1]):
        def double(cur, bit=bit):
            mine = (idx // bit) % 2
            def finish(other):
                first = jnp.where(mine == 0, cur, other)
                second = jnp.where(mine == 0, other, cur)
                return jnp.concatenate([first, second], axis=0)
            return cur, finish
        steps.append((bit, double))
    return [(bit, fn, [(i, i ^ bit) for i in range(n)]) for bit, fn in steps]


def fit_kernel(w_ref, cov_ref, a_ref, h_ref, o_ref):
    npred = cov_ref.shape[0]
    nint = cov_ref.shape[1] // H
    count = a_ref.shape[2]

    def row(p, r, cols):
        if r < 2:
            return h_ref[p, 0, pl.ds(r, 1), cols]
        if r < count + 2:
            return a_ref[p, 0, pl.ds(r - 2, 1), cols]
        return h_ref[p, 0, pl.ds(r - count, 1), cols]

    for s in range(TN // L):
        cols = pl.ds(s * L, L)
        w = [w_ref[d] for d in range(4)]
        for m in range(nint):
            rows = pl.ds(m * H, H)

            def body(p, acc):
                surf = w[0] * row(p, m + 1, cols)
                for d in range(1, 4):
                    surf = surf + w[d] * row(p, m + 1 + d, cols)
                return acc + cov_ref[p, rows, cols].astype(jnp.float32) * surf

            acc = lax.fori_loop(0, npred, body, jnp.zeros((H, L), jnp.float32), unroll=True)
            o_ref[rows, cols] = acc


def back_kernel(w_ref, cov_ref, t_ref, y_ref, g_ref, *rest):
    o_ref, rw_ref = rest[-2], rest[-1]
    npred = cov_ref.shape[0]
    nint = cov_ref.shape[1] // H
    for s in range(TN // L):
        cols = pl.ds(s * L, L)
        for m in range(nint):
            rows = pl.ds(m * H, H)
            resid = g_ref[rows, cols].astype(jnp.float32) * (y_ref[rows, cols] - t_ref[rows, cols])
            for d in range(4):
                rw_ref[d, rows, :] = w_ref[d] * resid

        def body(p, carry):
            o_ref[p, 0, pl.ds(0, 1), cols] = jnp.zeros((1, L), jnp.float32)
            accs = {}
            for m in range(nint):
                c = cov_ref[p, pl.ds(m * H, H), cols].astype(jnp.float32)
                for d in range(4):
                    prod = c * rw_ref[d, pl.ds(m * H, H), :]
                    half = prod[0:8] + prod[8:16]
                    r = m + 1 + d
                    accs[r] = half if r not in accs else accs[r] + half
                done = m + 1
                o_ref[p, 0, pl.ds(done, 1), cols] = jnp.sum(accs.pop(done), axis=0, keepdims=True)
            for r in sorted(accs):
                o_ref[p, 0, pl.ds(r, 1), cols] = jnp.sum(accs[r], axis=0, keepdims=True)
            return carry

        lax.fori_loop(0, npred, body, 0)


def fit_chunk(wl, cov, along, halo, chunk, width):
    npred, rows, _ = cov.shape
    count = along.shape[2]
    nh = halo.shape[2]
    off = chunk * (width // TN)
    return pl.pallas_call(
        fit_kernel,
        grid=(width // TN,),
        in_specs=[
            pl.BlockSpec((4, H, L), lambda j: (0, 0, 0)),
            pl.BlockSpec((npred, rows, TN), lambda j: (0, 0, j + off)),
            pl.BlockSpec((npred, 1, count, TN), lambda j: (0, j + off, 0, 0)),
            pl.BlockSpec((npred, 1, nh, TN), lambda j: (0, j + off, 0, 0)),
        ],
        out_specs=pl.BlockSpec((rows, TN), lambda j: (0, j)),
        out_shape=jax.ShapeDtypeStruct((rows, width), jnp.float32),
        compiler_params=pltpu.CompilerParams(dimension_semantics=("arbitrary",)),
        cost_estimate=pl.CostEstimate(
            flops=10 * npred * rows * width,
            transcendentals=0,
            bytes_accessed=2 * npred * rows * width + 4 * npred * (count + nh) * width + 4 * rows * width,
        ),
    )(wl, cov, along, halo)


def back_chunk(wl, cov, total, target, land, chunk, nrow, buf):
    npred, rows, ny = cov.shape
    width = total.shape[1]
    off = chunk * (width // TN)
    in_specs = [
        pl.BlockSpec((4, H, L), lambda j: (0, 0, 0)),
        pl.BlockSpec((npred, rows, TN), lambda j: (0, 0, j + off)),
        pl.BlockSpec((rows, TN), lambda j: (0, j)),
        pl.BlockSpec((rows, TN), lambda j: (0, j + off)),
        pl.BlockSpec((rows, TN), lambda j: (0, j + off)),
    ]
    args = [wl, cov, total, target, land]
    aliases = {}
    if buf is not None:
        in_specs.append(pl.BlockSpec(memory_space=pl.ANY))
        args.append(buf)
        aliases = {len(args) - 1: 0}
    return pl.pallas_call(
        back_kernel,
        grid=(width // TN,),
        in_specs=in_specs,
        out_specs=pl.BlockSpec((npred, 1, nrow, TN), lambda j: (0, j + off, 0, 0)),
        out_shape=jax.ShapeDtypeStruct((npred, ny // TN, nrow, TN), jnp.float32),
        scratch_shapes=[pltpu.VMEM((4, rows, L), jnp.float32)],
        input_output_aliases=aliases,
        compiler_params=pltpu.CompilerParams(dimension_semantics=("arbitrary",)),
        cost_estimate=pl.CostEstimate(
            flops=10 * npred * rows * width,
            transcendentals=0,
            bytes_accessed=2 * npred * rows * width + 12 * rows * width + 4 * npred * nrow * width,
        ),
    )(*args)


def penalty(padded, count):
    stencil = [1.0, -4.0, 6.0, -4.0, 1.0]
    along_rows = None
    for ii in range(5):
        term = stencil[ii] * padded[..., ii : ii + count, :]
        along_rows = term if along_rows is None else along_rows + term
    centre = padded[..., 2 : count + 2, :]
    width = centre.shape[-1]
    wide = jnp.pad(centre, [(0, 0)] * (centre.ndim - 1) + [(2, 2)])
    for ii in range(5):
        along_rows = along_rows + stencil[ii] * wide[..., ii : ii + width]
    return along_rows


def local(covariates, target, land, coefs, first_moment, second_moment, smoothing):
    npred, rows, ny = covariates.shape
    count = coefs.shape[1]
    knots = coefs.shape[2]
    share = rows // lax.axis_size("pred")
    start = lax.axis_index("pred") * share
    wl = jnp.broadcast_to(weight_table(H)[:, :, None], (4, H, L))
    peers = lax.axis_size("tile")
    up = [(i, i + 1) for i in range(peers - 1)]
    down = [(j, i) for i, j in up]
    before = lax.ppermute(coefs[:, count - 2 :], "tile", up)
    after = lax.ppermute(coefs[:, :2], "tile", down)
    padded = jnp.concatenate([before, coefs, after], axis=1)
    along = banded_along(coefs, ny)
    halo_along = banded_along(jnp.concatenate([before, after], axis=1), ny)
    nrow = padded.shape[1]
    target_blk = lax.dynamic_slice_in_dim(target, start, share, 0)
    land_blk = lax.dynamic_slice_in_dim(land, start, share, 0).astype(jnp.float32)
    width = ny // CHUNKS
    steps = reduce_steps(jnp.zeros((rows, width), jnp.float32), "pred")
    nsteps = len(steps)
    state = [None] * CHUNKS
    fitted_parts = [None] * CHUNKS
    back = None
    state[0] = fit_chunk(wl, covariates, along, halo_along, 0, width)
    next_back = 0
    for s in range(1, CHUNKS + nsteps + 1):
        pending = []
        for c in range(CHUNKS):
            k = s - c - 1
            if 0 <= k < nsteps:
                _, fn, pairs = steps[k]
                send, finish = fn(state[c])
                pending.append((c, finish, lax.ppermute(send, "pred", pairs)))
        outs = []
        if s < CHUNKS:
            outs.append(("fit", s, fit_chunk(wl, covariates, along, halo_along, s, width)))
        if next_back < CHUNKS and next_back + nsteps + 1 <= s:
            c = next_back
            outs.append(("back", c, back_chunk(wl, covariates, state[c], target, land, c, nrow, back)))
            next_back += 1
        recvs = [r for _, _, r in pending]
        if outs:
            recvs, vals = lax.optimization_barrier((recvs, [v for _, _, v in outs]))
            for (kind, c, _), v in zip(outs, vals):
                if kind == "fit":
                    state[c] = v
                else:
                    back = v
        for (c, finish, _), r in zip(pending, recvs):
            state[c] = finish(r)
    for c in range(CHUNKS):
        if c >= next_back:
            back = back_chunk(wl, covariates, state[c], target, land, c, nrow, back)
        fitted_parts[c] = lax.dynamic_slice_in_dim(state[c], start, share, 0)
    fitted = jnp.concatenate(fitted_parts, axis=1)
    residual = land_blk * (target_blk - fitted)
    grad_pad = -(1.0 / H) * banded_data(back, knots)
    inner = grad_pad[:, 2 : count + 2]
    from_below = from_behind(grad_pad[:, count + 2 :], "tile", 1)
    from_above = from_behind(grad_pad[:, :2], "tile", -1)
    middle = jnp.zeros((inner.shape[0], count - 2, inner.shape[2]), jnp.float32)
    low_add = jnp.concatenate([from_below, middle], axis=1)
    high_add = jnp.concatenate([middle, from_above], axis=1)
    data = inner + low_add + high_add
    gradient = data + smoothing[:, None, None] * penalty(padded, count)
    new_first = 0.9 * first_moment + 0.1 * gradient
    new_second = 0.99 * second_moment + 0.01 * gradient * gradient
    new_coefs = coefs - 0.1 * new_first / (jnp.sqrt(new_second) + 1e-08)
    return (fitted, residual, gradient, new_coefs, new_first, new_second)


def solution(mesh):
    in_specs = (
        P("pred", "tile", None),
        P("tile", None),
        P("tile", None),
        P("pred", "tile", None),
        P("pred", "tile", None),
        P("pred", "tile", None),
        P("pred"),
    )
    out_specs = (
        P(("tile", "pred"), None),
        P(("tile", "pred"), None),
        P("pred", "tile", None),
        P("pred", "tile", None),
        P("pred", "tile", None),
        P("pred", "tile", None),
    )
    return jax.shard_map(local, mesh=mesh, in_specs=in_specs, out_specs=out_specs, check_vma=False)
```

```python
import jax
import jax.numpy as jnp
from jax import lax
from jax.experimental import pallas as pl
from jax.experimental.pallas import tpu as pltpu
from jax.sharding import PartitionSpec as P

H = 16
TN = 512
L = 256
CHUNKS = 4
LEAD = 8


def extended(array, sides, width):
    for axis, dim in sides:
        peers, length = (lax.axis_size(axis), array.shape[dim])
        up = [(i, (i + 1) % peers) for i in range(peers - 1)]
        down = [(j, i) for i, j in up]
        last = lax.slice_in_dim(array, length - width, length, axis=dim)
        first = lax.slice_in_dim(array, 0, width, axis=dim)
        before = lax.ppermute(last, axis, up)
        after = lax.ppermute(first, axis, down)
        array = jnp.concatenate([before, array, after], axis=dim)
    return array


def from_behind(block, axis, distance):
    devices = range(lax.axis_size(axis))
    route = [(i - distance, i) for i in devices if i - distance in devices]
    return lax.ppermute(block, axis, route)


def weights_of(u):
    return [
        (1.0 - u) * (1.0 - u) * (1.0 - u) / 6.0,
        (3.0 * u * u * u - 6.0 * u * u + 4.0) / 6.0,
        (-3.0 * u * u * u + 3.0 * u * u + 3.0 * u + 1.0) / 6.0,
        u * u * u / 6.0,
    ]


def weight_table(spacing):
    u = (jnp.arange(spacing, dtype=jnp.float32) + 0.5) / spacing
    return jnp.stack(weights_of(u))


def block_basis(window):
    n = jnp.arange(window, dtype=jnp.int32)[:, None]
    j = jnp.arange(TN, dtype=jnp.int32)[None, :]
    u = ((j % H).astype(jnp.float32) + 0.5) / H
    values = weights_of(u)
    offset = n - LEAD + 1 - j // H
    basis = jnp.zeros((window, TN), jnp.float32)
    for dd in range(4):
        basis = jnp.where(offset == dd, values[dd], basis)
    return basis


def banded_along(padded, ny):
    knots = padded.shape[-1]
    per_block = TN // H
    window = 4 * per_block
    blocks = ny // TN
    right = per_block * (blocks - 1) + window - knots - LEAD
    cpad = jnp.pad(padded, ((0, 0), (0, 0), (LEAD, right)))
    cwin = jnp.stack([cpad[..., per_block * b : per_block * b + window] for b in range(blocks)], axis=1)
    return jnp.einsum("pbkn,nj->pbkj", cwin, block_basis(window), precision=lax.Precision.HIGH)


def banded_data(back4, knots):
    npred, blocks, nrow, _ = back4.shape
    per_block = TN // H
    window = 4 * per_block
    dwin = jnp.einsum("pbkj,nj->pkbn", back4, block_basis(window), precision=lax.Precision.HIGH)
    total = None
    for a in range(4):
        part = dwin[..., a * per_block : (a + 1) * per_block]
        part = jnp.pad(part, ((0, 0), (0, 0), (a, 3 - a), (0, 0)))
        total = part if total is None else total + part
    total = total.reshape(npred, nrow, (blocks + 3) * per_block)
    return total[..., LEAD : LEAD + knots]


def reduce_steps(x, axis):
    n = lax.axis_size(axis)
    idx = lax.axis_index(axis)
    bits = []
    bit = 1
    while bit < n:
        bits.append(bit)
        bit *= 2
    steps = []
    for bit in bits[:-1]:
        def halve(cur, bit=bit):
            half = cur.shape[0] // 2
            mine = (idx // bit) % 2
            pair = cur.reshape((2, half) + cur.shape[1:])
            keep = lax.dynamic_index_in_dim(pair, mine, 0, keepdims=False)
            send = lax.dynamic_index_in_dim(pair, 1 - mine, 0, keepdims=False)
            return send, lambda recv: keep + recv
        steps.append((bit, halve))
    for bit in bits[-1:]:
        def swap(cur):
            return cur, lambda recv: cur + recv
        steps.append((bit, swap))
    for bit in reversed(bits[1:-1]):
        def double(cur, bit=bit):
            mine = (idx // bit) % 2
            def finish(other):
                first = jnp.where(mine == 0, cur, other)
                second = jnp.where(mine == 0, other, cur)
                return jnp.concatenate([first, second], axis=0)
            return cur, finish
        steps.append((bit, double))
    if len(bits) > 1:
        def last(cur):
            return cur, lambda other: (cur, other)
        steps.append((1, last))
    return [(bit, fn, [(i, i ^ bit) for i in range(n)]) for bit, fn in steps]


def fit_kernel(w_ref, cov_ref, a_ref, o_ref):
    npred = cov_ref.shape[0]
    nint = cov_ref.shape[1] // H
    for s in range(TN // L):
        cols = pl.ds(s * L, L)
        w = [w_ref[d] for d in range(4)]
        for m in range(nint):
            rows = pl.ds(m * H, H)

            def body(p, acc):
                surf = w[0] * a_ref[p, 0, pl.ds(m + 1, 1), cols]
                for d in range(1, 4):
                    surf = surf + w[d] * a_ref[p, 0, pl.ds(m + 1 + d, 1), cols]
                return acc + cov_ref[p, rows, cols].astype(jnp.float32) * surf

            acc = lax.fori_loop(0, npred, body, jnp.zeros((H, L), jnp.float32), unroll=True)
            o_ref[rows, cols] = acc


def back_kernel(b_ref, w_ref, cov_ref, t_ref, u_ref, y_ref, g_ref, o_ref, rw_ref):
    npred = cov_ref.shape[0]
    nint = cov_ref.shape[1] // H
    mine = b_ref[0]
    for s in range(TN // L):
        cols = pl.ds(s * L, L)
        for m in range(nint):
            rows = pl.ds(m * H, H)
            inner = pl.ds((m % (nint // 2)) * H, H)
            side = m // (nint // 2)
            total = jnp.where(mine == side, t_ref[inner, cols], u_ref[inner, cols])
            resid = g_ref[rows, cols].astype(jnp.float32) * (y_ref[rows, cols] - total)
            for d in range(4):
                rw_ref[d, rows, :] = w_ref[d] * resid

        def body(p, carry):
            o_ref[p, 0, pl.ds(0, 1), cols] = jnp.zeros((1, L), jnp.float32)
            accs = {}
            for m in range(nint):
                c = cov_ref[p, pl.ds(m * H, H), cols].astype(jnp.float32)
                for d in range(4):
                    prod = c * rw_ref[d, pl.ds(m * H, H), :]
                    half = prod[0:8] + prod[8:16]
                    r = m + 1 + d
                    accs[r] = half if r not in accs else accs[r] + half
                done = m + 1
                o_ref[p, 0, pl.ds(done, 1), cols] = jnp.sum(accs.pop(done), axis=0, keepdims=True)
            for r in sorted(accs):
                o_ref[p, 0, pl.ds(r, 1), cols] = jnp.sum(accs[r], axis=0, keepdims=True)
            return carry

        lax.fori_loop(0, npred, body, 0)


def fit_chunk(wl, cov, along, chunk, width):
    npred, rows, _ = cov.shape
    nrow = along.shape[2]
    off = chunk * (width // TN)
    return pl.pallas_call(
        fit_kernel,
        grid=(width // TN,),
        in_specs=[
            pl.BlockSpec((4, H, L), lambda j: (0, 0, 0)),
            pl.BlockSpec((npred, rows, TN), lambda j: (0, 0, j + off)),
            pl.BlockSpec((npred, 1, nrow, TN), lambda j: (0, j + off, 0, 0)),
        ],
        out_specs=pl.BlockSpec((rows, TN), lambda j: (0, j)),
        out_shape=jax.ShapeDtypeStruct((rows, width), jnp.float32),
        compiler_params=pltpu.CompilerParams(dimension_semantics=("arbitrary",)),
        cost_estimate=pl.CostEstimate(
            flops=10 * npred * rows * width,
            transcendentals=0,
            bytes_accessed=2 * npred * rows * width + 4 * npred * nrow * width + 4 * rows * width,
        ),
    )(wl, cov, along)


def back_chunk(wl, cov, halves, target, land, chunk, nrow):
    npred, rows, _ = cov.shape
    cur, other, mine = halves
    width = cur.shape[1]
    off = chunk * (width // TN)
    return pl.pallas_call(
        back_kernel,
        grid=(width // TN,),
        in_specs=[
            pl.BlockSpec(memory_space=pltpu.SMEM),
            pl.BlockSpec((4, H, L), lambda j: (0, 0, 0)),
            pl.BlockSpec((npred, rows, TN), lambda j: (0, 0, j + off)),
            pl.BlockSpec((rows // 2, TN), lambda j: (0, j)),
            pl.BlockSpec((rows // 2, TN), lambda j: (0, j)),
            pl.BlockSpec((rows, TN), lambda j: (0, j + off)),
            pl.BlockSpec((rows, TN), lambda j: (0, j + off)),
        ],
        out_specs=pl.BlockSpec((npred, 1, nrow, TN), lambda j: (0, j, 0, 0)),
        out_shape=jax.ShapeDtypeStruct((npred, width // TN, nrow, TN), jnp.float32),
        scratch_shapes=[pltpu.VMEM((4, rows, L), jnp.float32)],
        compiler_params=pltpu.CompilerParams(dimension_semantics=("arbitrary",)),
        cost_estimate=pl.CostEstimate(
            flops=10 * npred * rows * width,
            transcendentals=0,
            bytes_accessed=2 * npred * rows * width + 12 * rows * width + 4 * npred * nrow * width,
        ),
    )(mine, wl, cov, cur, other, target, land)


def penalty(padded, count):
    stencil = [1.0, -4.0, 6.0, -4.0, 1.0]
    along_rows = None
    for ii in range(5):
        term = stencil[ii] * padded[..., ii : ii + count, :]
        along_rows = term if along_rows is None else along_rows + term
    centre = padded[..., 2 : count + 2, :]
    width = centre.shape[-1]
    wide = jnp.pad(centre, [(0, 0)] * (centre.ndim - 1) + [(2, 2)])
    for ii in range(5):
        along_rows = along_rows + stencil[ii] * wide[..., ii : ii + width]
    return along_rows


def local(covariates, target, land, coefs, first_moment, second_moment, smoothing):
    npred, rows, ny = covariates.shape
    count = coefs.shape[1]
    knots = coefs.shape[2]
    share = rows // lax.axis_size("pred")
    start = lax.axis_index("pred") * share
    wl = jnp.broadcast_to(weight_table(H)[:, :, None], (4, H, L))
    padded = extended(coefs, (("tile", 1),), 2)
    along = banded_along(padded, ny)
    nrow = padded.shape[1]
    target_blk = lax.dynamic_slice_in_dim(target, start, share, 0)
    land_blk = lax.dynamic_slice_in_dim(land, start, share, 0).astype(jnp.float32)
    width = ny // CHUNKS
    steps = reduce_steps(jnp.zeros((rows, width), jnp.float32), "pred")
    bit0 = lax.axis_index("pred") % 2
    bits_arr = jnp.reshape(bit0, (1,)).astype(jnp.int32)

    def attach(halves):
        return (halves[0], halves[1], bits_arr)

    nsteps = len(steps)
    state = [None] * CHUNKS
    fitted_parts = [None] * CHUNKS
    back_parts = [None] * CHUNKS
    state[0] = fit_chunk(wl, covariates, along, 0, width)
    next_back = 0
    for s in range(1, CHUNKS + nsteps + 1):
        pending = []
        for c in range(CHUNKS):
            k = s - c - 1
            if 0 <= k < nsteps:
                _, fn, pairs = steps[k]
                send, finish = fn(state[c])
                pending.append((c, finish, lax.ppermute(send, "pred", pairs)))
        outs = []
        if s < CHUNKS:
            outs.append(("fit", s, fit_chunk(wl, covariates, along, s, width)))
        if next_back < CHUNKS and next_back + nsteps + 1 <= s:
            c = next_back
            state[c] = attach(state[c])
            outs.append(("back", c, back_chunk(wl, covariates, state[c], target, land, c, nrow)))
            next_back += 1
        recvs = [r for _, _, r in pending]
        if outs:
            recvs, vals = lax.optimization_barrier((recvs, [v for _, _, v in outs]))
            for (kind, c, _), v in zip(outs, vals):
                if kind == "fit":
                    state[c] = v
                else:
                    back_parts[c] = v
        for (c, finish, _), r in zip(pending, recvs):
            state[c] = finish(r)
    for c in range(CHUNKS):
        if back_parts[c] is None:
            state[c] = attach(state[c])
            back_parts[c] = back_chunk(wl, covariates, state[c], target, land, c, nrow)
        cur, other, _ = state[c]
        half = rows // 2
        side = start // half
        picked = jnp.where(bit0 == side, cur, other)
        fitted_parts[c] = lax.dynamic_slice_in_dim(picked, start - side * half, share, 0)
    fitted = jnp.concatenate(fitted_parts, axis=1)
    residual = land_blk * (target_blk - fitted)
    back = jnp.concatenate(back_parts, axis=1)
    grad_pad = -(1.0 / H) * banded_data(back, knots)
    inner = grad_pad[:, 2 : count + 2]
    from_below = from_behind(grad_pad[:, count + 2 :], "tile", 1)
    from_above = from_behind(grad_pad[:, :2], "tile", -1)
    middle = jnp.zeros((inner.shape[0], count - 2, inner.shape[2]), jnp.float32)
    low_add = jnp.concatenate([from_below, middle], axis=1)
    high_add = jnp.concatenate([middle, from_above], axis=1)
    data = inner + low_add + high_add
    gradient = data + smoothing[:, None, None] * penalty(padded, count)
    new_first = 0.9 * first_moment + 0.1 * gradient
    new_second = 0.99 * second_moment + 0.01 * gradient * gradient
    new_coefs = coefs - 0.1 * new_first / (jnp.sqrt(new_second) + 1e-08)
    return (fitted, residual, gradient, new_coefs, new_first, new_second)


def solution(mesh):
    in_specs = (
        P("pred", "tile", None),
        P("tile", None),
        P("tile", None),
        P("pred", "tile", None),
        P("pred", "tile", None),
        P("pred", "tile", None),
        P("pred"),
    )
    out_specs = (
        P(("tile", "pred"), None),
        P(("tile", "pred"), None),
        P("pred", "tile", None),
        P("pred", "tile", None),
        P("pred", "tile", None),
        P("pred", "tile", None),
    )
    return jax.shard_map(local, mesh=mesh, in_specs=in_specs, out_specs=out_specs, check_vma=False)
```

```python
import jax
import jax.numpy as jnp
from jax import lax
from jax.experimental import pallas as pl
from jax.experimental.pallas import tpu as pltpu
from jax.sharding import PartitionSpec as P

H = 16
TN = 512
L = 256
CHUNKS = 4
LEAD = 8


def extended(array, sides, width):
    for axis, dim in sides:
        peers, length = (lax.axis_size(axis), array.shape[dim])
        up = [(i, (i + 1) % peers) for i in range(peers - 1)]
        down = [(j, i) for i, j in up]
        last = lax.slice_in_dim(array, length - width, length, axis=dim)
        first = lax.slice_in_dim(array, 0, width, axis=dim)
        before = lax.ppermute(last, axis, up)
        after = lax.ppermute(first, axis, down)
        array = jnp.concatenate([before, array, after], axis=dim)
    return array


def from_behind(block, axis, distance):
    devices = range(lax.axis_size(axis))
    route = [(i - distance, i) for i in devices if i - distance in devices]
    return lax.ppermute(block, axis, route)


def weights_of(u):
    return [
        (1.0 - u) * (1.0 - u) * (1.0 - u) / 6.0,
        (3.0 * u * u * u - 6.0 * u * u + 4.0) / 6.0,
        (-3.0 * u * u * u + 3.0 * u * u + 3.0 * u + 1.0) / 6.0,
        u * u * u / 6.0,
    ]


def weight_table(spacing):
    u = (jnp.arange(spacing, dtype=jnp.float32) + 0.5) / spacing
    return jnp.stack(weights_of(u))


def block_basis(window):
    n = jnp.arange(window, dtype=jnp.int32)[:, None]
    j = jnp.arange(TN, dtype=jnp.int32)[None, :]
    u = ((j % H).astype(jnp.float32) + 0.5) / H
    values = weights_of(u)
    offset = n - LEAD + 1 - j // H
    basis = jnp.zeros((window, TN), jnp.float32)
    for dd in range(4):
        basis = jnp.where(offset == dd, values[dd], basis)
    return basis


def banded_along(padded, ny):
    knots = padded.shape[-1]
    per_block = TN // H
    window = 4 * per_block
    blocks = ny // TN
    right = per_block * (blocks - 1) + window - knots - LEAD
    cpad = jnp.pad(padded, ((0, 0), (0, 0), (LEAD, right)))
    cwin = jnp.stack([cpad[..., per_block * b : per_block * b + window] for b in range(blocks)], axis=1)
    return jnp.einsum("pbkn,nj->pbkj", cwin, block_basis(window), precision=lax.Precision.HIGH)


def banded_data(back4, knots):
    npred, blocks, nrow, _ = back4.shape
    per_block = TN // H
    window = 4 * per_block
    dwin = jnp.einsum("pbkj,nj->pkbn", back4, block_basis(window), precision=lax.Precision.HIGH)
    total = None
    for a in range(4):
        part = dwin[..., a * per_block : (a + 1) * per_block]
        part = jnp.pad(part, ((0, 0), (0, 0), (a, 3 - a), (0, 0)))
        total = part if total is None else total + part
    total = total.reshape(npred, nrow, (blocks + 3) * per_block)
    return total[..., LEAD : LEAD + knots]


def reduce_steps(x, axis):
    n = lax.axis_size(axis)
    idx = lax.axis_index(axis)
    bits = []
    bit = 1
    while bit < n:
        bits.append(bit)
        bit *= 2
    steps = []
    for bit in bits[:-1]:
        def halve(cur, bit=bit):
            half = cur.shape[0] // 2
            mine = (idx // bit) % 2
            pair = cur.reshape((2, half) + cur.shape[1:])
            keep = lax.dynamic_index_in_dim(pair, mine, 0, keepdims=False)
            send = lax.dynamic_index_in_dim(pair, 1 - mine, 0, keepdims=False)
            return send, lambda recv: keep + recv
        steps.append((bit, halve))
    for bit in bits[-1:]:
        def swap(cur):
            return cur, lambda recv: cur + recv
        steps.append((bit, swap))
    for bit in reversed(bits[1:-1]):
        def double(cur, bit=bit):
            mine = (idx // bit) % 2
            def finish(other):
                first = jnp.where(mine == 0, cur, other)
                second = jnp.where(mine == 0, other, cur)
                return jnp.concatenate([first, second], axis=0)
            return cur, finish
        steps.append((bit, double))
    if len(bits) > 1:
        def last(cur):
            return cur, lambda other: (cur, other)
        steps.append((1, last))
    return [(bit, fn, [(i, i ^ bit) for i in range(n)]) for bit, fn in steps]


def fit_kernel(w_ref, cov_ref, a_ref, o_ref):
    npred = cov_ref.shape[0]
    nint = cov_ref.shape[1] // H
    for s in range(TN // L):
        cols = pl.ds(s * L, L)
        w = [w_ref[d] for d in range(4)]
        for m in range(nint):
            rows = pl.ds(m * H, H)

            def body(p, acc):
                surf = w[0] * a_ref[p, 0, pl.ds(m + 1, 1), cols]
                for d in range(1, 4):
                    surf = surf + w[d] * a_ref[p, 0, pl.ds(m + 1 + d, 1), cols]
                return acc + cov_ref[p, rows, cols].astype(jnp.float32) * surf

            acc = lax.fori_loop(0, npred, body, jnp.zeros((H, L), jnp.float32), unroll=True)
            o_ref[rows, cols] = acc


def back_kernel(b_ref, w_ref, cov_ref, t_ref, u_ref, y_ref, g_ref, o_ref, rw_ref):
    npred = cov_ref.shape[0]
    nint = cov_ref.shape[1] // H
    mine = b_ref[0]
    for s in range(TN // L):
        cols = pl.ds(s * L, L)
        for m in range(nint):
            rows = pl.ds(m * H, H)
            inner = pl.ds((m % (nint // 2)) * H, H)
            side = m // (nint // 2)
            total = jnp.where(mine == side, t_ref[inner, cols], u_ref[inner, cols])
            resid = g_ref[rows, cols].astype(jnp.float32) * (y_ref[rows, cols] - total)
            for d in range(4):
                rw_ref[d, rows, :] = w_ref[d] * resid

        def body(p, carry):
            o_ref[p, 0, pl.ds(0, 1), cols] = jnp.zeros((1, L), jnp.float32)
            accs = {}
            for m in range(nint):
                c = cov_ref[p, pl.ds(m * H, H), cols].astype(jnp.float32)
                for d in range(4):
                    prod = c * rw_ref[d, pl.ds(m * H, H), :]
                    half = prod[0:8] + prod[8:16]
                    r = m + 1 + d
                    accs[r] = half if r not in accs else accs[r] + half
                done = m + 1
                o_ref[p, 0, pl.ds(done, 1), cols] = jnp.sum(accs.pop(done), axis=0, keepdims=True)
            for r in sorted(accs):
                o_ref[p, 0, pl.ds(r, 1), cols] = jnp.sum(accs[r], axis=0, keepdims=True)
            return carry

        lax.fori_loop(0, npred, body, 0, unroll=2 if npred % 2 == 0 else 1)


def fit_chunk(wl, cov, along, chunk, width):
    npred, rows, _ = cov.shape
    nrow = along.shape[2]
    off = chunk * (width // TN)
    return pl.pallas_call(
        fit_kernel,
        grid=(width // TN,),
        in_specs=[
            pl.BlockSpec((4, H, L), lambda j: (0, 0, 0)),
            pl.BlockSpec((npred, rows, TN), lambda j: (0, 0, j + off)),
            pl.BlockSpec((npred, 1, nrow, TN), lambda j: (0, j + off, 0, 0)),
        ],
        out_specs=pl.BlockSpec((rows, TN), lambda j: (0, j)),
        out_shape=jax.ShapeDtypeStruct((rows, width), jnp.float32),
        compiler_params=pltpu.CompilerParams(dimension_semantics=("arbitrary",)),
        cost_estimate=pl.CostEstimate(
            flops=10 * npred * rows * width,
            transcendentals=0,
            bytes_accessed=2 * npred * rows * width + 4 * npred * nrow * width + 4 * rows * width,
        ),
    )(wl, cov, along)


def back_chunk(wl, cov, halves, target, land, chunk, nrow):
    npred, rows, _ = cov.shape
    cur, other, mine = halves
    width = cur.shape[1]
    off = chunk * (width // TN)
    return pl.pallas_call(
        back_kernel,
        grid=(width // TN,),
        in_specs=[
            pl.BlockSpec(memory_space=pltpu.SMEM),
            pl.BlockSpec((4, H, L), lambda j: (0, 0, 0)),
            pl.BlockSpec((npred, rows, TN), lambda j: (0, 0, j + off)),
            pl.BlockSpec((rows // 2, TN), lambda j: (0, j)),
            pl.BlockSpec((rows // 2, TN), lambda j: (0, j)),
            pl.BlockSpec((rows, TN), lambda j: (0, j + off)),
            pl.BlockSpec((rows, TN), lambda j: (0, j + off)),
        ],
        out_specs=pl.BlockSpec((npred, 1, nrow, TN), lambda j: (0, j, 0, 0)),
        out_shape=jax.ShapeDtypeStruct((npred, width // TN, nrow, TN), jnp.float32),
        scratch_shapes=[pltpu.VMEM((4, rows, L), jnp.float32)],
        compiler_params=pltpu.CompilerParams(dimension_semantics=("arbitrary",)),
        cost_estimate=pl.CostEstimate(
            flops=10 * npred * rows * width,
            transcendentals=0,
            bytes_accessed=2 * npred * rows * width + 12 * rows * width + 4 * npred * nrow * width,
        ),
    )(mine, wl, cov, cur, other, target, land)


def penalty(padded, count):
    stencil = [1.0, -4.0, 6.0, -4.0, 1.0]
    along_rows = None
    for ii in range(5):
        term = stencil[ii] * padded[..., ii : ii + count, :]
        along_rows = term if along_rows is None else along_rows + term
    centre = padded[..., 2 : count + 2, :]
    width = centre.shape[-1]
    wide = jnp.pad(centre, [(0, 0)] * (centre.ndim - 1) + [(2, 2)])
    for ii in range(5):
        along_rows = along_rows + stencil[ii] * wide[..., ii : ii + width]
    return along_rows


def local(covariates, target, land, coefs, first_moment, second_moment, smoothing):
    npred, rows, ny = covariates.shape
    count = coefs.shape[1]
    knots = coefs.shape[2]
    share = rows // lax.axis_size("pred")
    start = lax.axis_index("pred") * share
    wl = jnp.broadcast_to(weight_table(H)[:, :, None], (4, H, L))
    padded = extended(coefs, (("tile", 1),), 2)
    along = banded_along(padded, ny)
    nrow = padded.shape[1]
    target_blk = lax.dynamic_slice_in_dim(target, start, share, 0)
    land_blk = lax.dynamic_slice_in_dim(land, start, share, 0).astype(jnp.float32)
    width = ny // CHUNKS
    steps = reduce_steps(jnp.zeros((rows, width), jnp.float32), "pred")
    bit0 = lax.axis_index("pred") % 2
    bits_arr = jnp.reshape(bit0, (1,)).astype(jnp.int32)

    def attach(halves):
        return (halves[0], halves[1], bits_arr)

    nsteps = len(steps)
    state = [None] * CHUNKS
    fitted_parts = [None] * CHUNKS
    back_parts = [None] * CHUNKS
    state[0] = fit_chunk(wl, covariates, along, 0, width)
    next_back = 0
    for s in range(1, CHUNKS + nsteps + 1):
        pending = []
        for c in range(CHUNKS):
            k = s - c - 1
            if 0 <= k < nsteps:
                _, fn, pairs = steps[k]
                send, finish = fn(state[c])
                pending.append((c, finish, lax.ppermute(send, "pred", pairs)))
        outs = []
        if s < CHUNKS:
            outs.append(("fit", s, fit_chunk(wl, covariates, along, s, width)))
        if next_back < CHUNKS and next_back + nsteps + 1 <= s:
            c = next_back
            state[c] = attach(state[c])
            outs.append(("back", c, back_chunk(wl, covariates, state[c], target, land, c, nrow)))
            next_back += 1
        recvs = [r for _, _, r in pending]
        if outs:
            recvs, vals = lax.optimization_barrier((recvs, [v for _, _, v in outs]))
            for (kind, c, _), v in zip(outs, vals):
                if kind == "fit":
                    state[c] = v
                else:
                    back_parts[c] = v
        for (c, finish, _), r in zip(pending, recvs):
            state[c] = finish(r)
    for c in range(CHUNKS):
        if back_parts[c] is None:
            state[c] = attach(state[c])
            back_parts[c] = back_chunk(wl, covariates, state[c], target, land, c, nrow)
        cur, other, _ = state[c]
        half = rows // 2
        side = start // half
        picked = jnp.where(bit0 == side, cur, other)
        fitted_parts[c] = lax.dynamic_slice_in_dim(picked, start - side * half, share, 0)
    fitted = jnp.concatenate(fitted_parts, axis=1)
    residual = land_blk * (target_blk - fitted)
    back = jnp.concatenate(back_parts, axis=1)
    grad_pad = -(1.0 / H) * banded_data(back, knots)
    inner = grad_pad[:, 2 : count + 2]
    from_below = from_behind(grad_pad[:, count + 2 :], "tile", 1)
    from_above = from_behind(grad_pad[:, :2], "tile", -1)
    middle = jnp.zeros((inner.shape[0], count - 2, inner.shape[2]), jnp.float32)
    low_add = jnp.concatenate([from_below, middle], axis=1)
    high_add = jnp.concatenate([middle, from_above], axis=1)
    data = inner + low_add + high_add
    gradient = data + smoothing[:, None, None] * penalty(padded, count)
    new_first = 0.9 * first_moment + 0.1 * gradient
    new_second = 0.99 * second_moment + 0.01 * gradient * gradient
    new_coefs = coefs - 0.1 * new_first / (jnp.sqrt(new_second) + 1e-08)
    return (fitted, residual, gradient, new_coefs, new_first, new_second)


def solution(mesh):
    in_specs = (
        P("pred", "tile", None),
        P("tile", None),
        P("tile", None),
        P("pred", "tile", None),
        P("pred", "tile", None),
        P("pred", "tile", None),
        P("pred"),
    )
    out_specs = (
        P(("tile", "pred"), None),
        P(("tile", "pred"), None),
        P("pred", "tile", None),
        P("pred", "tile", None),
        P("pred", "tile", None),
        P("pred", "tile", None),
    )
    return jax.shard_map(local, mesh=mesh, in_specs=in_specs, out_specs=out_specs, check_vma=False)
```

```python
import jax
import jax.numpy as jnp
from jax import lax
from jax.experimental import pallas as pl
from jax.experimental.pallas import tpu as pltpu
from jax.sharding import PartitionSpec as P

H = 16
TN = 512
L = 256
CHUNKS = 4
LEAD = 8


def extended(array, sides, width):
    for axis, dim in sides:
        peers, length = (lax.axis_size(axis), array.shape[dim])
        up = [(i, (i + 1) % peers) for i in range(peers - 1)]
        down = [(j, i) for i, j in up]
        last = lax.slice_in_dim(array, length - width, length, axis=dim)
        first = lax.slice_in_dim(array, 0, width, axis=dim)
        before = lax.ppermute(last, axis, up)
        after = lax.ppermute(first, axis, down)
        array = jnp.concatenate([before, array, after], axis=dim)
    return array


def from_behind(block, axis, distance):
    devices = range(lax.axis_size(axis))
    route = [(i - distance, i) for i in devices if i - distance in devices]
    return lax.ppermute(block, axis, route)


def weights_of(u):
    return [
        (1.0 - u) * (1.0 - u) * (1.0 - u) / 6.0,
        (3.0 * u * u * u - 6.0 * u * u + 4.0) / 6.0,
        (-3.0 * u * u * u + 3.0 * u * u + 3.0 * u + 1.0) / 6.0,
        u * u * u / 6.0,
    ]


def weight_table(spacing):
    u = (jnp.arange(spacing, dtype=jnp.float32) + 0.5) / spacing
    return jnp.stack(weights_of(u))


def block_basis(window):
    n = jnp.arange(window, dtype=jnp.int32)[:, None]
    j = jnp.arange(TN, dtype=jnp.int32)[None, :]
    u = ((j % H).astype(jnp.float32) + 0.5) / H
    values = weights_of(u)
    offset = n - LEAD + 1 - j // H
    basis = jnp.zeros((window, TN), jnp.float32)
    for dd in range(4):
        basis = jnp.where(offset == dd, values[dd], basis)
    return basis


def banded_along(padded, ny):
    knots = padded.shape[-1]
    per_block = TN // H
    window = 4 * per_block
    blocks = ny // TN
    right = per_block * (blocks - 1) + window - knots - LEAD
    cpad = jnp.pad(padded, ((0, 0), (0, 0), (LEAD, right)))
    cwin = jnp.stack([cpad[..., per_block * b : per_block * b + window] for b in range(blocks)], axis=1)
    return jnp.einsum("pbkn,nj->pbkj", cwin, block_basis(window), precision=lax.Precision.HIGH)


def banded_data(parts, knots):
    npred, _, nrow, _ = parts[0].shape
    per_block = TN // H
    window = 4 * per_block
    basis = block_basis(window)
    dwin = jnp.concatenate(
        [jnp.einsum("pbkj,nj->pkbn", part, basis, precision=lax.Precision.HIGH) for part in parts], axis=2
    )
    blocks = dwin.shape[2]
    total = None
    for a in range(4):
        part = dwin[..., a * per_block : (a + 1) * per_block]
        part = jnp.pad(part, ((0, 0), (0, 0), (a, 3 - a), (0, 0)))
        total = part if total is None else total + part
    total = total.reshape(npred, nrow, (blocks + 3) * per_block)
    return total[..., LEAD : LEAD + knots]


def reduce_steps(x, axis):
    n = lax.axis_size(axis)
    idx = lax.axis_index(axis)
    bits = []
    bit = 1
    while bit < n:
        bits.append(bit)
        bit *= 2
    steps = []
    for bit in bits[:-1]:
        def halve(cur, bit=bit):
            half = cur.shape[0] // 2
            mine = (idx // bit) % 2
            pair = cur.reshape((2, half) + cur.shape[1:])
            keep = lax.dynamic_index_in_dim(pair, mine, 0, keepdims=False)
            send = lax.dynamic_index_in_dim(pair, 1 - mine, 0, keepdims=False)
            return send, lambda recv: keep + recv
        steps.append((bit, halve))
    for bit in bits[-1:]:
        def swap(cur):
            return cur, lambda recv: cur + recv
        steps.append((bit, swap))
    for bit in reversed(bits[1:-1]):
        def double(cur, bit=bit):
            mine = (idx // bit) % 2
            def finish(other):
                first = jnp.where(mine == 0, cur, other)
                second = jnp.where(mine == 0, other, cur)
                return jnp.concatenate([first, second], axis=0)
            return cur, finish
        steps.append((bit, double))
    if len(bits) > 1:
        def last(cur):
            return cur, lambda other: (cur, other)
        steps.append((1, last))
    return [(bit, fn, [(i, i ^ bit) for i in range(n)]) for bit, fn in steps]


def fit_kernel(w_ref, cov_ref, a_ref, o_ref):
    npred = cov_ref.shape[0]
    nint = cov_ref.shape[1] // H
    for s in range(TN // L):
        cols = pl.ds(s * L, L)
        w = [w_ref[d] for d in range(4)]
        for m in range(nint):
            rows = pl.ds(m * H, H)

            def body(p, acc):
                surf = w[0] * a_ref[p, 0, pl.ds(m + 1, 1), cols]
                for d in range(1, 4):
                    surf = surf + w[d] * a_ref[p, 0, pl.ds(m + 1 + d, 1), cols]
                return acc + cov_ref[p, rows, cols].astype(jnp.float32) * surf

            acc = lax.fori_loop(0, npred, body, jnp.zeros((H, L), jnp.float32), unroll=True)
            o_ref[rows, cols] = acc


def back_kernel(b_ref, w_ref, cov_ref, t_ref, u_ref, y_ref, g_ref, o_ref, rw_ref):
    npred = cov_ref.shape[0]
    nint = cov_ref.shape[1] // H
    mine = b_ref[0]
    for s in range(TN // L):
        cols = pl.ds(s * L, L)
        for m in range(nint):
            rows = pl.ds(m * H, H)
            inner = pl.ds((m % (nint // 2)) * H, H)
            side = m // (nint // 2)
            total = jnp.where(mine == side, t_ref[inner, cols], u_ref[inner, cols])
            resid = g_ref[rows, cols].astype(jnp.float32) * (y_ref[rows, cols] - total)
            for d in range(4):
                rw_ref[d, rows, :] = w_ref[d] * resid

        def body(p, carry):
            o_ref[p, 0, pl.ds(0, 1), cols] = jnp.zeros((1, L), jnp.float32)
            accs = {}
            for m in range(nint):
                c = cov_ref[p, pl.ds(m * H, H), cols].astype(jnp.float32)
                for d in range(4):
                    prod = c * rw_ref[d, pl.ds(m * H, H), :]
                    half = prod[0:8] + prod[8:16]
                    r = m + 1 + d
                    accs[r] = half if r not in accs else accs[r] + half
                done = m + 1
                o_ref[p, 0, pl.ds(done, 1), cols] = jnp.sum(accs.pop(done), axis=0, keepdims=True)
            for r in sorted(accs):
                o_ref[p, 0, pl.ds(r, 1), cols] = jnp.sum(accs[r], axis=0, keepdims=True)
            return carry

        lax.fori_loop(0, npred, body, 0, unroll=2 if npred % 2 == 0 else 1)


def fit_chunk(wl, cov, along, chunk, width):
    npred, rows, _ = cov.shape
    nrow = along.shape[2]
    off = chunk * (width // TN)
    return pl.pallas_call(
        fit_kernel,
        grid=(width // TN,),
        in_specs=[
            pl.BlockSpec((4, H, L), lambda j: (0, 0, 0)),
            pl.BlockSpec((npred, rows, TN), lambda j: (0, 0, j + off)),
            pl.BlockSpec((npred, 1, nrow, TN), lambda j: (0, j + off, 0, 0)),
        ],
        out_specs=pl.BlockSpec((rows, TN), lambda j: (0, j)),
        out_shape=jax.ShapeDtypeStruct((rows, width), jnp.float32),
        compiler_params=pltpu.CompilerParams(dimension_semantics=("arbitrary",)),
        cost_estimate=pl.CostEstimate(
            flops=10 * npred * rows * width,
            transcendentals=0,
            bytes_accessed=2 * npred * rows * width + 4 * npred * nrow * width + 4 * rows * width,
        ),
    )(wl, cov, along)


def back_chunk(wl, cov, halves, target, land, chunk, nrow):
    npred, rows, _ = cov.shape
    cur, other, mine = halves
    width = cur.shape[1]
    off = chunk * (width // TN)
    return pl.pallas_call(
        back_kernel,
        grid=(width // TN,),
        in_specs=[
            pl.BlockSpec(memory_space=pltpu.SMEM),
            pl.BlockSpec((4, H, L), lambda j: (0, 0, 0)),
            pl.BlockSpec((npred, rows, TN), lambda j: (0, 0, j + off)),
            pl.BlockSpec((rows // 2, TN), lambda j: (0, j)),
            pl.BlockSpec((rows // 2, TN), lambda j: (0, j)),
            pl.BlockSpec((rows, TN), lambda j: (0, j + off)),
            pl.BlockSpec((rows, TN), lambda j: (0, j + off)),
        ],
        out_specs=pl.BlockSpec((npred, 1, nrow, TN), lambda j: (0, j, 0, 0)),
        out_shape=jax.ShapeDtypeStruct((npred, width // TN, nrow, TN), jnp.float32),
        scratch_shapes=[pltpu.VMEM((4, rows, L), jnp.float32)],
        compiler_params=pltpu.CompilerParams(dimension_semantics=("arbitrary",)),
        cost_estimate=pl.CostEstimate(
            flops=10 * npred * rows * width,
            transcendentals=0,
            bytes_accessed=2 * npred * rows * width + 12 * rows * width + 4 * npred * nrow * width,
        ),
    )(mine, wl, cov, cur, other, target, land)


def penalty(padded, count):
    stencil = [1.0, -4.0, 6.0, -4.0, 1.0]
    along_rows = None
    for ii in range(5):
        term = stencil[ii] * padded[..., ii : ii + count, :]
        along_rows = term if along_rows is None else along_rows + term
    centre = padded[..., 2 : count + 2, :]
    width = centre.shape[-1]
    wide = jnp.pad(centre, [(0, 0)] * (centre.ndim - 1) + [(2, 2)])
    for ii in range(5):
        along_rows = along_rows + stencil[ii] * wide[..., ii : ii + width]
    return along_rows


def local(covariates, target, land, coefs, first_moment, second_moment, smoothing):
    npred, rows, ny = covariates.shape
    count = coefs.shape[1]
    knots = coefs.shape[2]
    share = rows // lax.axis_size("pred")
    start = lax.axis_index("pred") * share
    wl = jnp.broadcast_to(weight_table(H)[:, :, None], (4, H, L))
    padded = extended(coefs, (("tile", 1),), 2)
    along = banded_along(padded, ny)
    nrow = padded.shape[1]
    target_blk = lax.dynamic_slice_in_dim(target, start, share, 0)
    land_blk = lax.dynamic_slice_in_dim(land, start, share, 0).astype(jnp.float32)
    width = ny // CHUNKS
    steps = reduce_steps(jnp.zeros((rows, width), jnp.float32), "pred")
    bit0 = lax.axis_index("pred") % 2
    bits_arr = jnp.reshape(bit0, (1,)).astype(jnp.int32)

    def attach(halves):
        return (halves[0], halves[1], bits_arr)

    nsteps = len(steps)
    state = [None] * CHUNKS
    fitted_parts = [None] * CHUNKS
    back_parts = [None] * CHUNKS
    state[0] = fit_chunk(wl, covariates, along, 0, width)
    next_back = 0
    for s in range(1, CHUNKS + nsteps + 1):
        pending = []
        for c in range(CHUNKS):
            k = s - c - 1
            if 0 <= k < nsteps:
                _, fn, pairs = steps[k]
                send, finish = fn(state[c])
                pending.append((c, finish, lax.ppermute(send, "pred", pairs)))
        outs = []
        if s < CHUNKS:
            outs.append(("fit", s, fit_chunk(wl, covariates, along, s, width)))
        if next_back < CHUNKS and next_back + nsteps + 1 <= s:
            c = next_back
            state[c] = attach(state[c])
            outs.append(("back", c, back_chunk(wl, covariates, state[c], target, land, c, nrow)))
            next_back += 1
        recvs = [r for _, _, r in pending]
        if outs:
            recvs, vals = lax.optimization_barrier((recvs, [v for _, _, v in outs]))
            for (kind, c, _), v in zip(outs, vals):
                if kind == "fit":
                    state[c] = v
                else:
                    back_parts[c] = v
        for (c, finish, _), r in zip(pending, recvs):
            state[c] = finish(r)
    for c in range(CHUNKS):
        if back_parts[c] is None:
            state[c] = attach(state[c])
            back_parts[c] = back_chunk(wl, covariates, state[c], target, land, c, nrow)
        cur, other, _ = state[c]
        half = rows // 2
        side = start // half
        picked = jnp.where(bit0 == side, cur, other)
        fitted_parts[c] = lax.dynamic_slice_in_dim(picked, start - side * half, share, 0)
    fitted = jnp.concatenate(fitted_parts, axis=1)
    residual = land_blk * (target_blk - fitted)
    grad_pad = -(1.0 / H) * banded_data(back_parts, knots)
    inner = grad_pad[:, 2 : count + 2]
    from_below = from_behind(grad_pad[:, count + 2 :], "tile", 1)
    from_above = from_behind(grad_pad[:, :2], "tile", -1)
    middle = jnp.zeros((inner.shape[0], count - 2, inner.shape[2]), jnp.float32)
    low_add = jnp.concatenate([from_below, middle], axis=1)
    high_add = jnp.concatenate([middle, from_above], axis=1)
    data = inner + low_add + high_add
    gradient = data + smoothing[:, None, None] * penalty(padded, count)
    new_first = 0.9 * first_moment + 0.1 * gradient
    new_second = 0.99 * second_moment + 0.01 * gradient * gradient
    new_coefs = coefs - 0.1 * new_first / (jnp.sqrt(new_second) + 1e-08)
    return (fitted, residual, gradient, new_coefs, new_first, new_second)


def solution(mesh):
    in_specs = (
        P("pred", "tile", None),
        P("tile", None),
        P("tile", None),
        P("pred", "tile", None),
        P("pred", "tile", None),
        P("pred", "tile", None),
        P("pred"),
    )
    out_specs = (
        P(("tile", "pred"), None),
        P(("tile", "pred"), None),
        P("pred", "tile", None),
        P("pred", "tile", None),
        P("pred", "tile", None),
        P("pred", "tile", None),
    )
    return jax.shard_map(local, mesh=mesh, in_specs=in_specs, out_specs=out_specs, check_vma=False)
```

```python
import jax
import jax.numpy as jnp
from jax import lax
from jax.experimental import pallas as pl
from jax.experimental.pallas import tpu as pltpu
from jax.sharding import PartitionSpec as P

H = 16
TN = 512
L = 256
CHUNKS = 4
LEAD = 8


def extended(array, sides, width):
    for axis, dim in sides:
        peers, length = (lax.axis_size(axis), array.shape[dim])
        up = [(i, (i + 1) % peers) for i in range(peers - 1)]
        down = [(j, i) for i, j in up]
        last = lax.slice_in_dim(array, length - width, length, axis=dim)
        first = lax.slice_in_dim(array, 0, width, axis=dim)
        before = lax.ppermute(last, axis, up)
        after = lax.ppermute(first, axis, down)
        array = jnp.concatenate([before, array, after], axis=dim)
    return array


def from_behind(block, axis, distance):
    devices = range(lax.axis_size(axis))
    route = [(i - distance, i) for i in devices if i - distance in devices]
    return lax.ppermute(block, axis, route)


def weights_of(u):
    return [
        (1.0 - u) * (1.0 - u) * (1.0 - u) / 6.0,
        (3.0 * u * u * u - 6.0 * u * u + 4.0) / 6.0,
        (-3.0 * u * u * u + 3.0 * u * u + 3.0 * u + 1.0) / 6.0,
        u * u * u / 6.0,
    ]


def weight_table(spacing):
    u = (jnp.arange(spacing, dtype=jnp.float32) + 0.5) / spacing
    return jnp.stack(weights_of(u))


def block_basis(window):
    n = jnp.arange(window, dtype=jnp.int32)[:, None]
    j = jnp.arange(TN, dtype=jnp.int32)[None, :]
    u = ((j % H).astype(jnp.float32) + 0.5) / H
    values = weights_of(u)
    offset = n - LEAD + 1 - j // H
    basis = jnp.zeros((window, TN), jnp.float32)
    for dd in range(4):
        basis = jnp.where(offset == dd, values[dd], basis)
    return basis


def banded_along(padded, ny):
    knots = padded.shape[-1]
    per_block = TN // H
    window = 4 * per_block
    blocks = ny // TN
    right = per_block * (blocks - 1) + window - knots - LEAD
    cpad = jnp.pad(padded, ((0, 0), (0, 0), (LEAD, right)))
    cwin = jnp.stack([cpad[..., per_block * b : per_block * b + window] for b in range(blocks)], axis=1)
    return jnp.einsum("pbkn,nj->pbkj", cwin, block_basis(window), precision=lax.Precision.HIGH)


def banded_data(parts, knots):
    npred, _, nrow, _ = parts[0].shape
    per_block = TN // H
    window = 4 * per_block
    basis = block_basis(window)
    dwin = jnp.concatenate(
        [jnp.einsum("pbkj,nj->pkbn", part, basis, precision=lax.Precision.HIGH) for part in parts], axis=2
    )
    blocks = dwin.shape[2]
    total = None
    for a in range(4):
        part = dwin[..., a * per_block : (a + 1) * per_block]
        part = jnp.pad(part, ((0, 0), (0, 0), (a, 3 - a), (0, 0)))
        total = part if total is None else total + part
    total = total.reshape(npred, nrow, (blocks + 3) * per_block)
    return total[..., LEAD : LEAD + knots]


def reduce_steps(x, axis):
    n = lax.axis_size(axis)
    idx = lax.axis_index(axis)
    bits = []
    bit = 1
    while bit < n:
        bits.append(bit)
        bit *= 2
    steps = []
    for bit in bits[:-1]:
        def halve(cur, bit=bit):
            half = cur.shape[0] // 2
            mine = (idx // bit) % 2
            pair = cur.reshape((2, half) + cur.shape[1:])
            keep = lax.dynamic_index_in_dim(pair, mine, 0, keepdims=False)
            send = lax.dynamic_index_in_dim(pair, 1 - mine, 0, keepdims=False)
            return send, lambda recv: keep + recv
        steps.append((bit, halve))
    for bit in bits[-1:]:
        def swap(cur):
            return cur, lambda recv: cur + recv
        steps.append((bit, swap))
    for bit in reversed(bits[1:-1]):
        def double(cur, bit=bit):
            mine = (idx // bit) % 2
            def finish(other):
                first = jnp.where(mine == 0, cur, other)
                second = jnp.where(mine == 0, other, cur)
                return jnp.concatenate([first, second], axis=0)
            return cur, finish
        steps.append((bit, double))
    if len(bits) > 1:
        def last(cur):
            return cur, lambda other: (cur, other)
        steps.append((1, last))
    return [(bit, fn, [(i, i ^ bit) for i in range(n)]) for bit, fn in steps]


def fit_kernel(w_ref, cov_ref, a_ref, o_ref):
    npred = cov_ref.shape[0]
    nint = cov_ref.shape[1] // H
    for s in range(TN // L):
        cols = pl.ds(s * L, L)
        w = [w_ref[d] for d in range(4)]
        for m in range(nint):
            rows = pl.ds(m * H, H)

            def body(p, acc):
                surf = w[0] * a_ref[p, 0, pl.ds(m + 1, 1), cols]
                for d in range(1, 4):
                    surf = surf + w[d] * a_ref[p, 0, pl.ds(m + 1 + d, 1), cols]
                return acc + cov_ref[p, rows, cols].astype(jnp.float32) * surf

            acc = lax.fori_loop(0, npred, body, jnp.zeros((H, L), jnp.float32), unroll=True)
            o_ref[rows, cols] = acc


def back_kernel(b_ref, w_ref, cov_ref, t_ref, u_ref, y_ref, g_ref, o_ref, rw_ref):
    npred = cov_ref.shape[0]
    nint = cov_ref.shape[1] // H
    mine = b_ref[0]
    for s in range(TN // L):
        cols = pl.ds(s * L, L)
        for m in range(nint):
            rows = pl.ds(m * H, H)
            inner = pl.ds((m % (nint // 2)) * H, H)
            side = m // (nint // 2)
            total = jnp.where(mine == side, t_ref[inner, cols], u_ref[inner, cols])
            resid = g_ref[rows, cols].astype(jnp.float32) * (y_ref[rows, cols] - total)
            for d in range(4):
                rw_ref[d, rows, :] = w_ref[d] * resid

        def body(p, carry):
            o_ref[p, 0, pl.ds(0, 1), cols] = jnp.zeros((1, L), jnp.float32)
            accs = {}
            for m in range(nint):
                c = cov_ref[p, pl.ds(m * H, H), cols].astype(jnp.float32)
                for d in range(4):
                    prod = c * rw_ref[d, pl.ds(m * H, H), :]
                    half = prod[0:8] + prod[8:16]
                    r = m + 1 + d
                    accs[r] = half if r not in accs else accs[r] + half
                done = m + 1
                o_ref[p, 0, pl.ds(done, 1), cols] = jnp.sum(accs.pop(done), axis=0, keepdims=True)
            for r in sorted(accs):
                o_ref[p, 0, pl.ds(r, 1), cols] = jnp.sum(accs[r], axis=0, keepdims=True)
            return carry

        lax.fori_loop(0, npred, body, 0, unroll=2 if npred % 2 == 0 else 1)


def fit_chunk(wl, cov, along, off, width):
    npred, rows, _ = cov.shape
    nrow = along.shape[2]
    return pl.pallas_call(
        fit_kernel,
        grid=(width // TN,),
        in_specs=[
            pl.BlockSpec((4, H, L), lambda j: (0, 0, 0)),
            pl.BlockSpec((npred, rows, TN), lambda j: (0, 0, j + off)),
            pl.BlockSpec((npred, 1, nrow, TN), lambda j: (0, j + off, 0, 0)),
        ],
        out_specs=pl.BlockSpec((rows, TN), lambda j: (0, j)),
        out_shape=jax.ShapeDtypeStruct((rows, width), jnp.float32),
        compiler_params=pltpu.CompilerParams(dimension_semantics=("arbitrary",)),
        cost_estimate=pl.CostEstimate(
            flops=10 * npred * rows * width,
            transcendentals=0,
            bytes_accessed=2 * npred * rows * width + 4 * npred * nrow * width + 4 * rows * width,
        ),
    )(wl, cov, along)


def back_chunk(wl, cov, halves, target, land, off, nrow):
    npred, rows, _ = cov.shape
    cur, other, mine = halves
    width = cur.shape[1]
    return pl.pallas_call(
        back_kernel,
        grid=(width // TN,),
        in_specs=[
            pl.BlockSpec(memory_space=pltpu.SMEM),
            pl.BlockSpec((4, H, L), lambda j: (0, 0, 0)),
            pl.BlockSpec((npred, rows, TN), lambda j: (0, 0, j + off)),
            pl.BlockSpec((rows // 2, TN), lambda j: (0, j)),
            pl.BlockSpec((rows // 2, TN), lambda j: (0, j)),
            pl.BlockSpec((rows, TN), lambda j: (0, j + off)),
            pl.BlockSpec((rows, TN), lambda j: (0, j + off)),
        ],
        out_specs=pl.BlockSpec((npred, 1, nrow, TN), lambda j: (0, j, 0, 0)),
        out_shape=jax.ShapeDtypeStruct((npred, width // TN, nrow, TN), jnp.float32),
        scratch_shapes=[pltpu.VMEM((4, rows, L), jnp.float32)],
        compiler_params=pltpu.CompilerParams(dimension_semantics=("arbitrary",)),
        cost_estimate=pl.CostEstimate(
            flops=10 * npred * rows * width,
            transcendentals=0,
            bytes_accessed=2 * npred * rows * width + 12 * rows * width + 4 * npred * nrow * width,
        ),
    )(mine, wl, cov, cur, other, target, land)


def penalty(padded, count):
    stencil = [1.0, -4.0, 6.0, -4.0, 1.0]
    along_rows = None
    for ii in range(5):
        term = stencil[ii] * padded[..., ii : ii + count, :]
        along_rows = term if along_rows is None else along_rows + term
    centre = padded[..., 2 : count + 2, :]
    width = centre.shape[-1]
    wide = jnp.pad(centre, [(0, 0)] * (centre.ndim - 1) + [(2, 2)])
    for ii in range(5):
        along_rows = along_rows + stencil[ii] * wide[..., ii : ii + width]
    return along_rows


def local(covariates, target, land, coefs, first_moment, second_moment, smoothing):
    npred, rows, ny = covariates.shape
    count = coefs.shape[1]
    knots = coefs.shape[2]
    share = rows // lax.axis_size("pred")
    start = lax.axis_index("pred") * share
    wl = jnp.broadcast_to(weight_table(H)[:, :, None], (4, H, L))
    padded = extended(coefs, (("tile", 1),), 2)
    along = banded_along(padded, ny)
    nrow = padded.shape[1]
    target_blk = lax.dynamic_slice_in_dim(target, start, share, 0)
    land_blk = lax.dynamic_slice_in_dim(land, start, share, 0).astype(jnp.float32)
    blocks = ny // TN
    base = blocks // CHUNKS
    counts = [base] * CHUNKS
    if base >= 2 and CHUNKS >= 2 and blocks == base * CHUNKS:
        counts[0] -= 1
        counts[-1] += 1
    offs = [sum(counts[:c]) for c in range(CHUNKS)]
    widths = [n * TN for n in counts]
    width = widths[0]
    steps = reduce_steps(jnp.zeros((rows, width), jnp.float32), "pred")
    bit0 = lax.axis_index("pred") % 2
    bits_arr = jnp.reshape(bit0, (1,)).astype(jnp.int32)

    def attach(halves):
        return (halves[0], halves[1], bits_arr)

    nsteps = len(steps)
    state = [None] * CHUNKS
    fitted_parts = [None] * CHUNKS
    back_parts = [None] * CHUNKS
    state[0] = fit_chunk(wl, covariates, along, offs[0], widths[0])
    next_back = 0
    for s in range(1, CHUNKS + nsteps + 1):
        pending = []
        for c in range(CHUNKS):
            k = s - c - 1
            if 0 <= k < nsteps:
                _, fn, pairs = steps[k]
                send, finish = fn(state[c])
                pending.append((c, finish, lax.ppermute(send, "pred", pairs)))
        outs = []
        if s < CHUNKS:
            outs.append(("fit", s, fit_chunk(wl, covariates, along, offs[s], widths[s])))
        if next_back < CHUNKS and next_back + nsteps + 1 <= s:
            c = next_back
            state[c] = attach(state[c])
            outs.append(("back", c, back_chunk(wl, covariates, state[c], target, land, offs[c], nrow)))
            next_back += 1
        recvs = [r for _, _, r in pending]
        if outs:
            recvs, vals = lax.optimization_barrier((recvs, [v for _, _, v in outs]))
            for (kind, c, _), v in zip(outs, vals):
                if kind == "fit":
                    state[c] = v
                else:
                    back_parts[c] = v
        for (c, finish, _), r in zip(pending, recvs):
            state[c] = finish(r)
    for c in range(CHUNKS):
        if back_parts[c] is None:
            state[c] = attach(state[c])
            back_parts[c] = back_chunk(wl, covariates, state[c], target, land, offs[c], nrow)
        cur, other, _ = state[c]
        half = rows // 2
        side = start // half
        picked = jnp.where(bit0 == side, cur, other)
        fitted_parts[c] = lax.dynamic_slice_in_dim(picked, start - side * half, share, 0)
    fitted = jnp.concatenate(fitted_parts, axis=1)
    residual = land_blk * (target_blk - fitted)
    grad_pad = -(1.0 / H) * banded_data(back_parts, knots)
    inner = grad_pad[:, 2 : count + 2]
    from_below = from_behind(grad_pad[:, count + 2 :], "tile", 1)
    from_above = from_behind(grad_pad[:, :2], "tile", -1)
    middle = jnp.zeros((inner.shape[0], count - 2, inner.shape[2]), jnp.float32)
    low_add = jnp.concatenate([from_below, middle], axis=1)
    high_add = jnp.concatenate([middle, from_above], axis=1)
    data = inner + low_add + high_add
    gradient = data + smoothing[:, None, None] * penalty(padded, count)
    new_first = 0.9 * first_moment + 0.1 * gradient
    new_second = 0.99 * second_moment + 0.01 * gradient * gradient
    new_coefs = coefs - 0.1 * new_first / (jnp.sqrt(new_second) + 1e-08)
    return (fitted, residual, gradient, new_coefs, new_first, new_second)


def solution(mesh):
    in_specs = (
        P("pred", "tile", None),
        P("tile", None),
        P("tile", None),
        P("pred", "tile", None),
        P("pred", "tile", None),
        P("pred", "tile", None),
        P("pred"),
    )
    out_specs = (
        P(("tile", "pred"), None),
        P(("tile", "pred"), None),
        P("pred", "tile", None),
        P("pred", "tile", None),
        P("pred", "tile", None),
        P("pred", "tile", None),
    )
    return jax.shard_map(local, mesh=mesh, in_specs=in_specs, out_specs=out_specs, check_vma=False)
```

```python
import jax
import jax.numpy as jnp
from jax import lax
from jax.experimental import pallas as pl
from jax.experimental.pallas import tpu as pltpu
from jax.sharding import PartitionSpec as P

H = 16
TN = 512
L = 256
CHUNKS = 4
LEAD = 8


def extended(array, sides, width):
    for axis, dim in sides:
        peers, length = (lax.axis_size(axis), array.shape[dim])
        up = [(i, (i + 1) % peers) for i in range(peers - 1)]
        down = [(j, i) for i, j in up]
        last = lax.slice_in_dim(array, length - width, length, axis=dim)
        first = lax.slice_in_dim(array, 0, width, axis=dim)
        before = lax.ppermute(last, axis, up)
        after = lax.ppermute(first, axis, down)
        array = jnp.concatenate([before, array, after], axis=dim)
    return array


def from_behind(block, axis, distance):
    devices = range(lax.axis_size(axis))
    route = [(i - distance, i) for i in devices if i - distance in devices]
    return lax.ppermute(block, axis, route)


def weights_of(u):
    return [
        (1.0 - u) * (1.0 - u) * (1.0 - u) / 6.0,
        (3.0 * u * u * u - 6.0 * u * u + 4.0) / 6.0,
        (-3.0 * u * u * u + 3.0 * u * u + 3.0 * u + 1.0) / 6.0,
        u * u * u / 6.0,
    ]


def weight_table(spacing):
    u = (jnp.arange(spacing, dtype=jnp.float32) + 0.5) / spacing
    return jnp.stack(weights_of(u))


def block_basis(window):
    n = jnp.arange(window, dtype=jnp.int32)[:, None]
    j = jnp.arange(TN, dtype=jnp.int32)[None, :]
    u = ((j % H).astype(jnp.float32) + 0.5) / H
    values = weights_of(u)
    offset = n - LEAD + 1 - j // H
    basis = jnp.zeros((window, TN), jnp.float32)
    for dd in range(4):
        basis = jnp.where(offset == dd, values[dd], basis)
    return basis


def banded_along(padded, ny):
    knots = padded.shape[-1]
    per_block = TN // H
    window = 4 * per_block
    blocks = ny // TN
    right = per_block * (blocks - 1) + window - knots - LEAD
    cpad = jnp.pad(padded, ((0, 0), (0, 0), (LEAD, right)))
    cwin = jnp.stack([cpad[..., per_block * b : per_block * b + window] for b in range(blocks)], axis=1)
    return jnp.einsum("pbkn,nj->pbkj", cwin, block_basis(window), precision=lax.Precision.HIGH)


def banded_data(parts, knots):
    npred, _, nrow, _ = parts[0].shape
    per_block = TN // H
    window = 4 * per_block
    basis = block_basis(window)
    dwin = jnp.concatenate(
        [jnp.einsum("pbkj,nj->pkbn", part, basis, precision=lax.Precision.HIGH) for part in parts], axis=2
    )
    blocks = dwin.shape[2]
    total = None
    for a in range(4):
        part = dwin[..., a * per_block : (a + 1) * per_block]
        part = jnp.pad(part, ((0, 0), (0, 0), (a, 3 - a), (0, 0)))
        total = part if total is None else total + part
    total = total.reshape(npred, nrow, (blocks + 3) * per_block)
    return total[..., LEAD : LEAD + knots]


def reduce_steps(x, axis):
    n = lax.axis_size(axis)
    idx = lax.axis_index(axis)
    bits = []
    bit = 1
    while bit < n:
        bits.append(bit)
        bit *= 2
    steps = []
    for bit in bits[:-1]:
        def halve(cur, bit=bit):
            half = cur.shape[0] // 2
            mine = (idx // bit) % 2
            pair = cur.reshape((2, half) + cur.shape[1:])
            keep = lax.dynamic_index_in_dim(pair, mine, 0, keepdims=False)
            send = lax.dynamic_index_in_dim(pair, 1 - mine, 0, keepdims=False)
            return send, lambda recv: keep + recv
        steps.append((bit, halve))
    for bit in bits[-1:]:
        def swap(cur):
            return cur, lambda recv: cur + recv
        steps.append((bit, swap))
    for bit in reversed(bits[1:-1]):
        def double(cur, bit=bit):
            mine = (idx // bit) % 2
            def finish(other):
                first = jnp.where(mine == 0, cur, other)
                second = jnp.where(mine == 0, other, cur)
                return jnp.concatenate([first, second], axis=0)
            return cur, finish
        steps.append((bit, double))
    if len(bits) > 1:
        def last(cur):
            return cur, lambda other: (cur, other)
        steps.append((1, last))
    return [(bit, fn, [(i, i ^ bit) for i in range(n)]) for bit, fn in steps]


def fit_kernel(w_ref, cov_ref, a_ref, o_ref):
    npred = cov_ref.shape[0]
    nint = cov_ref.shape[1] // H
    for s in range(TN // L):
        cols = pl.ds(s * L, L)
        w = [w_ref[d] for d in range(4)]
        for m in range(nint):
            rows = pl.ds(m * H, H)

            def body(p, acc):
                surf = w[0] * a_ref[p, 0, pl.ds(m + 1, 1), cols]
                for d in range(1, 4):
                    surf = surf + w[d] * a_ref[p, 0, pl.ds(m + 1 + d, 1), cols]
                return acc + cov_ref[p, rows, cols].astype(jnp.float32) * surf

            acc = lax.fori_loop(0, npred, body, jnp.zeros((H, L), jnp.float32), unroll=True)
            o_ref[rows, cols] = acc


def back_kernel(b_ref, w_ref, cov_ref, t_ref, u_ref, y_ref, g_ref, o_ref, rw_ref):
    npred = cov_ref.shape[0]
    nint = cov_ref.shape[1] // H
    mine = b_ref[0]
    for s in range(TN // L):
        cols = pl.ds(s * L, L)
        for m in range(nint):
            rows = pl.ds(m * H, H)
            inner = pl.ds((m % (nint // 2)) * H, H)
            side = m // (nint // 2)
            total = jnp.where(mine == side, t_ref[inner, cols], u_ref[inner, cols])
            resid = g_ref[rows, cols].astype(jnp.float32) * (y_ref[rows, cols] - total)
            for d in range(4):
                rw_ref[d, rows, :] = w_ref[d] * resid

        def body(p, carry):
            o_ref[p, 0, pl.ds(0, 1), cols] = jnp.zeros((1, L), jnp.float32)
            accs = {}
            for m in range(nint):
                c = cov_ref[p, pl.ds(m * H, H), cols].astype(jnp.float32)
                for d in range(4):
                    prod = c * rw_ref[d, pl.ds(m * H, H), :]
                    half = prod[0:8] + prod[8:16]
                    r = m + 1 + d
                    accs[r] = half if r not in accs else accs[r] + half
                done = m + 1
                o_ref[p, 0, pl.ds(done, 1), cols] = jnp.sum(accs.pop(done), axis=0, keepdims=True)
            for r in sorted(accs):
                o_ref[p, 0, pl.ds(r, 1), cols] = jnp.sum(accs[r], axis=0, keepdims=True)
            return carry

        lax.fori_loop(0, npred, body, 0, unroll=4 if npred % 4 == 0 else 1)


def fit_chunk(wl, cov, along, off, width):
    npred, rows, _ = cov.shape
    nrow = along.shape[2]
    return pl.pallas_call(
        fit_kernel,
        grid=(width // TN,),
        in_specs=[
            pl.BlockSpec((4, H, L), lambda j: (0, 0, 0)),
            pl.BlockSpec((npred, rows, TN), lambda j: (0, 0, j + off)),
            pl.BlockSpec((npred, 1, nrow, TN), lambda j: (0, j + off, 0, 0)),
        ],
        out_specs=pl.BlockSpec((rows, TN), lambda j: (0, j)),
        out_shape=jax.ShapeDtypeStruct((rows, width), jnp.float32),
        compiler_params=pltpu.CompilerParams(dimension_semantics=("arbitrary",)),
        cost_estimate=pl.CostEstimate(
            flops=10 * npred * rows * width,
            transcendentals=0,
            bytes_accessed=2 * npred * rows * width + 4 * npred * nrow * width + 4 * rows * width,
        ),
    )(wl, cov, along)


def back_chunk(wl, cov, halves, target, land, off, nrow):
    npred, rows, _ = cov.shape
    cur, other, mine = halves
    width = cur.shape[1]
    return pl.pallas_call(
        back_kernel,
        grid=(width // TN,),
        in_specs=[
            pl.BlockSpec(memory_space=pltpu.SMEM),
            pl.BlockSpec((4, H, L), lambda j: (0, 0, 0)),
            pl.BlockSpec((npred, rows, TN), lambda j: (0, 0, j + off)),
            pl.BlockSpec((rows // 2, TN), lambda j: (0, j)),
            pl.BlockSpec((rows // 2, TN), lambda j: (0, j)),
            pl.BlockSpec((rows, TN), lambda j: (0, j + off)),
            pl.BlockSpec((rows, TN), lambda j: (0, j + off)),
        ],
        out_specs=pl.BlockSpec((npred, 1, nrow, TN), lambda j: (0, j, 0, 0)),
        out_shape=jax.ShapeDtypeStruct((npred, width // TN, nrow, TN), jnp.float32),
        scratch_shapes=[pltpu.VMEM((4, rows, L), jnp.float32)],
        compiler_params=pltpu.CompilerParams(dimension_semantics=("arbitrary",)),
        cost_estimate=pl.CostEstimate(
            flops=10 * npred * rows * width,
            transcendentals=0,
            bytes_accessed=2 * npred * rows * width + 12 * rows * width + 4 * npred * nrow * width,
        ),
    )(mine, wl, cov, cur, other, target, land)


def penalty(padded, count):
    stencil = [1.0, -4.0, 6.0, -4.0, 1.0]
    along_rows = None
    for ii in range(5):
        term = stencil[ii] * padded[..., ii : ii + count, :]
        along_rows = term if along_rows is None else along_rows + term
    centre = padded[..., 2 : count + 2, :]
    width = centre.shape[-1]
    wide = jnp.pad(centre, [(0, 0)] * (centre.ndim - 1) + [(2, 2)])
    for ii in range(5):
        along_rows = along_rows + stencil[ii] * wide[..., ii : ii + width]
    return along_rows


def local(covariates, target, land, coefs, first_moment, second_moment, smoothing):
    npred, rows, ny = covariates.shape
    count = coefs.shape[1]
    knots = coefs.shape[2]
    share = rows // lax.axis_size("pred")
    start = lax.axis_index("pred") * share
    wl = jnp.broadcast_to(weight_table(H)[:, :, None], (4, H, L))
    padded = extended(coefs, (("tile", 1),), 2)
    along = banded_along(padded, ny)
    nrow = padded.shape[1]
    target_blk = lax.dynamic_slice_in_dim(target, start, share, 0)
    land_blk = lax.dynamic_slice_in_dim(land, start, share, 0).astype(jnp.float32)
    blocks = ny // TN
    base = blocks // CHUNKS
    counts = [base] * CHUNKS
    if base >= 2 and CHUNKS >= 2 and blocks == base * CHUNKS:
        counts[0] -= 1
        counts[-1] += 1
    offs = [sum(counts[:c]) for c in range(CHUNKS)]
    widths = [n * TN for n in counts]
    width = widths[0]
    steps = reduce_steps(jnp.zeros((rows, width), jnp.float32), "pred")
    bit0 = lax.axis_index("pred") % 2
    bits_arr = jnp.reshape(bit0, (1,)).astype(jnp.int32)

    def attach(halves):
        return (halves[0], halves[1], bits_arr)

    nsteps = len(steps)
    state = [None] * CHUNKS
    fitted_parts = [None] * CHUNKS
    back_parts = [None] * CHUNKS
    state[0] = fit_chunk(wl, covariates, along, offs[0], widths[0])
    next_back = 0
    for s in range(1, CHUNKS + nsteps + 1):
        pending = []
        for c in range(CHUNKS):
            k = s - c - 1
            if 0 <= k < nsteps:
                _, fn, pairs = steps[k]
                send, finish = fn(state[c])
                pending.append((c, finish, lax.ppermute(send, "pred", pairs)))
        outs = []
        if s < CHUNKS:
            outs.append(("fit", s, fit_chunk(wl, covariates, along, offs[s], widths[s])))
        if next_back < CHUNKS and next_back + nsteps + 1 <= s:
            c = next_back
            state[c] = attach(state[c])
            outs.append(("back", c, back_chunk(wl, covariates, state[c], target, land, offs[c], nrow)))
            next_back += 1
        recvs = [r for _, _, r in pending]
        if outs:
            recvs, vals = lax.optimization_barrier((recvs, [v for _, _, v in outs]))
            for (kind, c, _), v in zip(outs, vals):
                if kind == "fit":
                    state[c] = v
                else:
                    back_parts[c] = v
        for (c, finish, _), r in zip(pending, recvs):
            state[c] = finish(r)
    for c in range(CHUNKS):
        if back_parts[c] is None:
            state[c] = attach(state[c])
            back_parts[c] = back_chunk(wl, covariates, state[c], target, land, offs[c], nrow)
        cur, other, _ = state[c]
        half = rows // 2
        side = start // half
        picked = jnp.where(bit0 == side, cur, other)
        fitted_parts[c] = lax.dynamic_slice_in_dim(picked, start - side * half, share, 0)
    fitted = jnp.concatenate(fitted_parts, axis=1)
    residual = land_blk * (target_blk - fitted)
    grad_pad = -(1.0 / H) * banded_data(back_parts, knots)
    inner = grad_pad[:, 2 : count + 2]
    from_below = from_behind(grad_pad[:, count + 2 :], "tile", 1)
    from_above = from_behind(grad_pad[:, :2], "tile", -1)
    middle = jnp.zeros((inner.shape[0], count - 2, inner.shape[2]), jnp.float32)
    low_add = jnp.concatenate([from_below, middle], axis=1)
    high_add = jnp.concatenate([middle, from_above], axis=1)
    data = inner + low_add + high_add
    gradient = data + smoothing[:, None, None] * penalty(padded, count)
    new_first = 0.9 * first_moment + 0.1 * gradient
    new_second = 0.99 * second_moment + 0.01 * gradient * gradient
    new_coefs = coefs - 0.1 * new_first / (jnp.sqrt(new_second) + 1e-08)
    return (fitted, residual, gradient, new_coefs, new_first, new_second)


def solution(mesh):
    in_specs = (
        P("pred", "tile", None),
        P("tile", None),
        P("tile", None),
        P("pred", "tile", None),
        P("pred", "tile", None),
        P("pred", "tile", None),
        P("pred"),
    )
    out_specs = (
        P(("tile", "pred"), None),
        P(("tile", "pred"), None),
        P("pred", "tile", None),
        P("pred", "tile", None),
        P("pred", "tile", None),
        P("pred", "tile", None),
    )
    return jax.shard_map(local, mesh=mesh, in_specs=in_specs, out_specs=out_specs, check_vma=False)
```

```python
import jax
import jax.numpy as jnp
from jax import lax
from jax.experimental import pallas as pl
from jax.experimental.pallas import tpu as pltpu
from jax.sharding import PartitionSpec as P

H = 16
TN = 512
L = 256
CHUNKS = 4
LEAD = 8


def extended(array, sides, width):
    for axis, dim in sides:
        peers, length = (lax.axis_size(axis), array.shape[dim])
        up = [(i, (i + 1) % peers) for i in range(peers - 1)]
        down = [(j, i) for i, j in up]
        last = lax.slice_in_dim(array, length - width, length, axis=dim)
        first = lax.slice_in_dim(array, 0, width, axis=dim)
        before = lax.ppermute(last, axis, up)
        after = lax.ppermute(first, axis, down)
        array = jnp.concatenate([before, array, after], axis=dim)
    return array


def from_behind(block, axis, distance):
    devices = range(lax.axis_size(axis))
    route = [(i - distance, i) for i in devices if i - distance in devices]
    return lax.ppermute(block, axis, route)


def weights_of(u):
    return [
        (1.0 - u) * (1.0 - u) * (1.0 - u) / 6.0,
        (3.0 * u * u * u - 6.0 * u * u + 4.0) / 6.0,
        (-3.0 * u * u * u + 3.0 * u * u + 3.0 * u + 1.0) / 6.0,
        u * u * u / 6.0,
    ]


def weight_table(spacing):
    u = (jnp.arange(spacing, dtype=jnp.float32) + 0.5) / spacing
    return jnp.stack(weights_of(u))


def block_basis(window):
    n = jnp.arange(window, dtype=jnp.int32)[:, None]
    j = jnp.arange(TN, dtype=jnp.int32)[None, :]
    u = ((j % H).astype(jnp.float32) + 0.5) / H
    values = weights_of(u)
    offset = n - LEAD + 1 - j // H
    basis = jnp.zeros((window, TN), jnp.float32)
    for dd in range(4):
        basis = jnp.where(offset == dd, values[dd], basis)
    return basis


def banded_along(padded, ny):
    knots = padded.shape[-1]
    per_block = TN // H
    window = 4 * per_block
    blocks = ny // TN
    right = per_block * (blocks - 1) + window - knots - LEAD
    cpad = jnp.pad(padded, ((0, 0), (0, 0), (LEAD, right)))
    cwin = jnp.stack([cpad[..., per_block * b : per_block * b + window] for b in range(blocks)], axis=1)
    return jnp.einsum("pbkn,nj->pbkj", cwin, block_basis(window), precision=lax.Precision.HIGH)


def banded_data(parts, knots):
    npred, _, nrow, _ = parts[0].shape
    per_block = TN // H
    window = 4 * per_block
    basis = block_basis(window)
    dwin = jnp.concatenate(
        [jnp.einsum("pbkj,nj->pkbn", part, basis, precision=lax.Precision.HIGH) for part in parts], axis=2
    )
    blocks = dwin.shape[2]
    total = None
    for a in range(4):
        part = dwin[..., a * per_block : (a + 1) * per_block]
        part = jnp.pad(part, ((0, 0), (0, 0), (a, 3 - a), (0, 0)))
        total = part if total is None else total + part
    total = total.reshape(npred, nrow, (blocks + 3) * per_block)
    return total[..., LEAD : LEAD + knots]


def reduce_steps(x, axis):
    n = lax.axis_size(axis)
    idx = lax.axis_index(axis)
    bits = []
    bit = 1
    while bit < n:
        bits.append(bit)
        bit *= 2
    steps = []
    for bit in bits[:-1]:
        def halve(cur, bit=bit):
            half = cur.shape[0] // 2
            mine = (idx // bit) % 2
            pair = cur.reshape((2, half) + cur.shape[1:])
            keep = lax.dynamic_index_in_dim(pair, mine, 0, keepdims=False)
            send = lax.dynamic_index_in_dim(pair, 1 - mine, 0, keepdims=False)
            return send, lambda recv: keep + recv
        steps.append((bit, halve))
    for bit in bits[-1:]:
        def swap(cur):
            return cur, lambda recv: cur + recv
        steps.append((bit, swap))
    for bit in reversed(bits[1:-1]):
        def double(cur, bit=bit):
            mine = (idx // bit) % 2
            def finish(other):
                first = jnp.where(mine == 0, cur, other)
                second = jnp.where(mine == 0, other, cur)
                return jnp.concatenate([first, second], axis=0)
            return cur, finish
        steps.append((bit, double))
    if len(bits) > 1:
        def last(cur):
            return cur, lambda other: (cur, other)
        steps.append((1, last))
    return [(bit, fn, [(i, i ^ bit) for i in range(n)]) for bit, fn in steps]


def kernel_weights():
    u = (lax.broadcasted_iota(jnp.int32, (H, L), 0).astype(jnp.float32) + 0.5) / H
    return weights_of(u)


def fit_kernel(cov_ref, a_ref, o_ref):
    npred = cov_ref.shape[0]
    nint = cov_ref.shape[1] // H
    for s in range(TN // L):
        cols = pl.ds(s * L, L)
        w = kernel_weights()
        for m in range(nint):
            rows = pl.ds(m * H, H)

            def body(p, acc):
                surf = w[0] * a_ref[p, 0, pl.ds(m + 1, 1), cols]
                for d in range(1, 4):
                    surf = surf + w[d] * a_ref[p, 0, pl.ds(m + 1 + d, 1), cols]
                return acc + cov_ref[p, rows, cols].astype(jnp.float32) * surf

            acc = lax.fori_loop(0, npred, body, jnp.zeros((H, L), jnp.float32), unroll=True)
            o_ref[rows, cols] = acc


def back_kernel(b_ref, cov_ref, t_ref, u_ref, y_ref, g_ref, o_ref, rw_ref):
    npred = cov_ref.shape[0]
    nint = cov_ref.shape[1] // H
    mine = b_ref[0]
    w = kernel_weights()
    for s in range(TN // L):
        cols = pl.ds(s * L, L)
        for m in range(nint):
            rows = pl.ds(m * H, H)
            inner = pl.ds((m % (nint // 2)) * H, H)
            side = m // (nint // 2)
            total = jnp.where(mine == side, t_ref[inner, cols], u_ref[inner, cols])
            resid = g_ref[rows, cols].astype(jnp.float32) * (y_ref[rows, cols] - total)
            for d in range(4):
                rw_ref[d, rows, :] = w[d] * resid

        def body(p, carry):
            o_ref[p, 0, pl.ds(0, 1), cols] = jnp.zeros((1, L), jnp.float32)
            accs = {}
            for m in range(nint):
                c = cov_ref[p, pl.ds(m * H, H), cols].astype(jnp.float32)
                for d in range(4):
                    prod = c * rw_ref[d, pl.ds(m * H, H), :]
                    half = prod[0:8] + prod[8:16]
                    r = m + 1 + d
                    accs[r] = half if r not in accs else accs[r] + half
                done = m + 1
                o_ref[p, 0, pl.ds(done, 1), cols] = jnp.sum(accs.pop(done), axis=0, keepdims=True)
            for r in sorted(accs):
                o_ref[p, 0, pl.ds(r, 1), cols] = jnp.sum(accs[r], axis=0, keepdims=True)
            return carry

        lax.fori_loop(0, npred, body, 0, unroll=4 if npred % 4 == 0 else 1)


def fit_chunk(cov, along, off, width):
    npred, rows, _ = cov.shape
    nrow = along.shape[2]
    return pl.pallas_call(
        fit_kernel,
        grid=(width // TN,),
        in_specs=[
            pl.BlockSpec((npred, rows, TN), lambda j: (0, 0, j + off)),
            pl.BlockSpec((npred, 1, nrow, TN), lambda j: (0, j + off, 0, 0)),
        ],
        out_specs=pl.BlockSpec((rows, TN), lambda j: (0, j)),
        out_shape=jax.ShapeDtypeStruct((rows, width), jnp.float32),
        compiler_params=pltpu.CompilerParams(dimension_semantics=("arbitrary",)),
        cost_estimate=pl.CostEstimate(
            flops=10 * npred * rows * width,
            transcendentals=0,
            bytes_accessed=2 * npred * rows * width + 4 * npred * nrow * width + 4 * rows * width,
        ),
    )(cov, along)


def back_chunk(cov, halves, target, land, off, nrow):
    npred, rows, _ = cov.shape
    cur, other, mine = halves
    width = cur.shape[1]
    return pl.pallas_call(
        back_kernel,
        grid=(width // TN,),
        in_specs=[
            pl.BlockSpec(memory_space=pltpu.SMEM),
            pl.BlockSpec((npred, rows, TN), lambda j: (0, 0, j + off)),
            pl.BlockSpec((rows // 2, TN), lambda j: (0, j)),
            pl.BlockSpec((rows // 2, TN), lambda j: (0, j)),
            pl.BlockSpec((rows, TN), lambda j: (0, j + off)),
            pl.BlockSpec((rows, TN), lambda j: (0, j + off)),
        ],
        out_specs=pl.BlockSpec((npred, 1, nrow, TN), lambda j: (0, j, 0, 0)),
        out_shape=jax.ShapeDtypeStruct((npred, width // TN, nrow, TN), jnp.float32),
        scratch_shapes=[pltpu.VMEM((4, rows, L), jnp.float32)],
        compiler_params=pltpu.CompilerParams(dimension_semantics=("arbitrary",)),
        cost_estimate=pl.CostEstimate(
            flops=10 * npred * rows * width,
            transcendentals=0,
            bytes_accessed=2 * npred * rows * width + 12 * rows * width + 4 * npred * nrow * width,
        ),
    )(mine, cov, cur, other, target, land)


def penalty(padded, count):
    stencil = [1.0, -4.0, 6.0, -4.0, 1.0]
    along_rows = None
    for ii in range(5):
        term = stencil[ii] * padded[..., ii : ii + count, :]
        along_rows = term if along_rows is None else along_rows + term
    centre = padded[..., 2 : count + 2, :]
    width = centre.shape[-1]
    wide = jnp.pad(centre, [(0, 0)] * (centre.ndim - 1) + [(2, 2)])
    for ii in range(5):
        along_rows = along_rows + stencil[ii] * wide[..., ii : ii + width]
    return along_rows


def local(covariates, target, land, coefs, first_moment, second_moment, smoothing):
    npred, rows, ny = covariates.shape
    count = coefs.shape[1]
    knots = coefs.shape[2]
    share = rows // lax.axis_size("pred")
    start = lax.axis_index("pred") * share
    padded = extended(coefs, (("tile", 1),), 2)
    along = banded_along(padded, ny)
    nrow = padded.shape[1]
    target_blk = lax.dynamic_slice_in_dim(target, start, share, 0)
    land_blk = lax.dynamic_slice_in_dim(land, start, share, 0).astype(jnp.float32)
    blocks = ny // TN
    base = blocks // CHUNKS
    counts = [base] * CHUNKS
    if base >= 2 and CHUNKS >= 2 and blocks == base * CHUNKS:
        counts[0] -= 1
        counts[-1] += 1
    offs = [sum(counts[:c]) for c in range(CHUNKS)]
    widths = [n * TN for n in counts]
    width = widths[0]
    steps = reduce_steps(jnp.zeros((rows, width), jnp.float32), "pred")
    bit0 = lax.axis_index("pred") % 2
    bits_arr = jnp.reshape(bit0, (1,)).astype(jnp.int32)

    def attach(halves):
        return (halves[0], halves[1], bits_arr)

    nsteps = len(steps)
    state = [None] * CHUNKS
    fitted_parts = [None] * CHUNKS
    back_parts = [None] * CHUNKS
    state[0] = fit_chunk(covariates, along, offs[0], widths[0])
    next_back = 0
    for s in range(1, CHUNKS + nsteps + 1):
        pending = []
        for c in range(CHUNKS):
            k = s - c - 1
            if 0 <= k < nsteps:
                _, fn, pairs = steps[k]
                send, finish = fn(state[c])
                pending.append((c, finish, lax.ppermute(send, "pred", pairs)))
        outs = []
        if s < CHUNKS:
            outs.append(("fit", s, fit_chunk(covariates, along, offs[s], widths[s])))
        if next_back < CHUNKS and next_back + nsteps + 1 <= s:
            c = next_back
            state[c] = attach(state[c])
            outs.append(("back", c, back_chunk(covariates, state[c], target, land, offs[c], nrow)))
            next_back += 1
        recvs = [r for _, _, r in pending]
        if outs:
            recvs, vals = lax.optimization_barrier((recvs, [v for _, _, v in outs]))
            for (kind, c, _), v in zip(outs, vals):
                if kind == "fit":
                    state[c] = v
                else:
                    back_parts[c] = v
        for (c, finish, _), r in zip(pending, recvs):
            state[c] = finish(r)
    for c in range(CHUNKS):
        if back_parts[c] is None:
            state[c] = attach(state[c])
            back_parts[c] = back_chunk(covariates, state[c], target, land, offs[c], nrow)
        cur, other, _ = state[c]
        half = rows // 2
        side = start // half
        picked = jnp.where(bit0 == side, cur, other)
        fitted_parts[c] = lax.dynamic_slice_in_dim(picked, start - side * half, share, 0)
    fitted = jnp.concatenate(fitted_parts, axis=1)
    residual = land_blk * (target_blk - fitted)
    grad_pad = -(1.0 / H) * banded_data(back_parts, knots)
    inner = grad_pad[:, 2 : count + 2]
    from_below = from_behind(grad_pad[:, count + 2 :], "tile", 1)
    from_above = from_behind(grad_pad[:, :2], "tile", -1)
    middle = jnp.zeros((inner.shape[0], count - 2, inner.shape[2]), jnp.float32)
    low_add = jnp.concatenate([from_below, middle], axis=1)
    high_add = jnp.concatenate([middle, from_above], axis=1)
    data = inner + low_add + high_add
    gradient = data + smoothing[:, None, None] * penalty(padded, count)
    new_first = 0.9 * first_moment + 0.1 * gradient
    new_second = 0.99 * second_moment + 0.01 * gradient * gradient
    new_coefs = coefs - 0.1 * new_first / (jnp.sqrt(new_second) + 1e-08)
    return (fitted, residual, gradient, new_coefs, new_first, new_second)


def solution(mesh):
    in_specs = (
        P("pred", "tile", None),
        P("tile", None),
        P("tile", None),
        P("pred", "tile", None),
        P("pred", "tile", None),
        P("pred", "tile", None),
        P("pred"),
    )
    out_specs = (
        P(("tile", "pred"), None),
        P(("tile", "pred"), None),
        P("pred", "tile", None),
        P("pred", "tile", None),
        P("pred", "tile", None),
        P("pred", "tile", None),
    )
    return jax.shard_map(local, mesh=mesh, in_specs=in_specs, out_specs=out_specs, check_vma=False)
```

```python
import jax
import jax.numpy as jnp
from jax import lax
from jax.experimental import pallas as pl
from jax.experimental.pallas import tpu as pltpu
from jax.sharding import PartitionSpec as P

H = 16
TN = 512
L = 256
CHUNKS = 4
LEAD = 8


def extended(array, sides, width):
    for axis, dim in sides:
        peers, length = (lax.axis_size(axis), array.shape[dim])
        up = [(i, (i + 1) % peers) for i in range(peers - 1)]
        down = [(j, i) for i, j in up]
        last = lax.slice_in_dim(array, length - width, length, axis=dim)
        first = lax.slice_in_dim(array, 0, width, axis=dim)
        before = lax.ppermute(last, axis, up)
        after = lax.ppermute(first, axis, down)
        array = jnp.concatenate([before, array, after], axis=dim)
    return array


def from_behind(block, axis, distance):
    devices = range(lax.axis_size(axis))
    route = [(i - distance, i) for i in devices if i - distance in devices]
    return lax.ppermute(block, axis, route)


def weights_of(u):
    return [
        (1.0 - u) * (1.0 - u) * (1.0 - u) / 6.0,
        (3.0 * u * u * u - 6.0 * u * u + 4.0) / 6.0,
        (-3.0 * u * u * u + 3.0 * u * u + 3.0 * u + 1.0) / 6.0,
        u * u * u / 6.0,
    ]


def weight_table(spacing):
    u = (jnp.arange(spacing, dtype=jnp.float32) + 0.5) / spacing
    return jnp.stack(weights_of(u))


def block_basis(window):
    n = jnp.arange(window, dtype=jnp.int32)[:, None]
    j = jnp.arange(TN, dtype=jnp.int32)[None, :]
    u = ((j % H).astype(jnp.float32) + 0.5) / H
    values = weights_of(u)
    offset = n - LEAD + 1 - j // H
    basis = jnp.zeros((window, TN), jnp.float32)
    for dd in range(4):
        basis = jnp.where(offset == dd, values[dd], basis)
    return basis


def banded_along(padded, ny):
    knots = padded.shape[-1]
    per_block = TN // H
    window = 4 * per_block
    blocks = ny // TN
    right = per_block * (blocks - 1) + window - knots - LEAD
    cpad = jnp.pad(padded, ((0, 0), (0, 0), (LEAD, right)))
    cwin = jnp.stack([cpad[..., per_block * b : per_block * b + window] for b in range(blocks)], axis=1)
    return jnp.einsum("pbkn,nj->pbkj", cwin, block_basis(window), precision=lax.Precision.HIGH)


def banded_data(parts, knots):
    npred, _, nrow, _ = parts[0].shape
    per_block = TN // H
    window = 4 * per_block
    basis = block_basis(window)
    dwin = jnp.concatenate(
        [jnp.einsum("pbkj,nj->pkbn", part, basis, precision=lax.Precision.HIGH) for part in parts], axis=2
    )
    blocks = dwin.shape[2]
    total = None
    for a in range(4):
        part = dwin[..., a * per_block : (a + 1) * per_block]
        part = jnp.pad(part, ((0, 0), (0, 0), (a, 3 - a), (0, 0)))
        total = part if total is None else total + part
    total = total.reshape(npred, nrow, (blocks + 3) * per_block)
    return total[..., LEAD : LEAD + knots]


def reduce_steps(x, axis):
    n = lax.axis_size(axis)
    idx = lax.axis_index(axis)
    bits = []
    bit = 1
    while bit < n:
        bits.append(bit)
        bit *= 2
    steps = []
    for bit in bits[:-1]:
        def halve(cur, bit=bit):
            half = cur.shape[0] // 2
            mine = (idx // bit) % 2
            pair = cur.reshape((2, half) + cur.shape[1:])
            keep = lax.dynamic_index_in_dim(pair, mine, 0, keepdims=False)
            send = lax.dynamic_index_in_dim(pair, 1 - mine, 0, keepdims=False)
            return send, lambda recv: keep + recv
        steps.append((bit, halve))
    for bit in bits[-1:]:
        def swap(cur):
            return cur, lambda recv: cur + recv
        steps.append((bit, swap))
    for bit in reversed(bits[1:-1]):
        def double(cur, bit=bit):
            mine = (idx // bit) % 2
            def finish(other):
                first = jnp.where(mine == 0, cur, other)
                second = jnp.where(mine == 0, other, cur)
                return jnp.concatenate([first, second], axis=0)
            return cur, finish
        steps.append((bit, double))
    if len(bits) > 1:
        def last(cur):
            return cur, lambda other: (cur, other)
        steps.append((1, last))
    return [(bit, fn, [(i, i ^ bit) for i in range(n)]) for bit, fn in steps]


def fit_kernel(w_ref, cov_ref, a_ref, o_ref):
    npred = cov_ref.shape[0]
    nint = cov_ref.shape[1] // H
    for s in range(TN // L):
        cols = pl.ds(s * L, L)
        w = [w_ref[d] for d in range(4)]
        for m in range(nint):
            rows = pl.ds(m * H, H)

            def body(p, acc):
                surf = w[0] * a_ref[p, 0, pl.ds(m + 1, 1), cols]
                for d in range(1, 4):
                    surf = surf + w[d] * a_ref[p, 0, pl.ds(m + 1 + d, 1), cols]
                return acc + cov_ref[p, rows, cols].astype(jnp.float32) * surf

            acc = lax.fori_loop(0, npred, body, jnp.zeros((H, L), jnp.float32), unroll=True)
            o_ref[rows, cols] = acc


def back_kernel(b_ref, w_ref, cov_ref, t_ref, u_ref, y_ref, g_ref, o_ref, rw_ref):
    npred = cov_ref.shape[0]
    nint = cov_ref.shape[1] // H
    mine = b_ref[0]
    for s in range(TN // L):
        cols = pl.ds(s * L, L)
        for m in range(nint):
            rows = pl.ds(m * H, H)
            inner = pl.ds((m % (nint // 2)) * H, H)
            side = m // (nint // 2)
            total = jnp.where(mine == side, t_ref[inner, cols], u_ref[inner, cols])
            resid = g_ref[rows, cols].astype(jnp.float32) * (y_ref[rows, cols] - total)
            for d in range(4):
                rw_ref[d, rows, :] = w_ref[d] * resid

        def body(p, carry):
            o_ref[p, 0, pl.ds(0, 1), cols] = jnp.zeros((1, L), jnp.float32)
            accs = {}
            for m in range(nint):
                c = cov_ref[p, pl.ds(m * H, H), cols].astype(jnp.float32)
                for d in range(4):
                    prod = c * rw_ref[d, pl.ds(m * H, H), :]
                    half = prod[0:8] + prod[8:16]
                    r = m + 1 + d
                    accs[r] = half if r not in accs else accs[r] + half
                done = m + 1
                o_ref[p, 0, pl.ds(done, 1), cols] = jnp.sum(accs.pop(done), axis=0, keepdims=True)
            for r in sorted(accs):
                o_ref[p, 0, pl.ds(r, 1), cols] = jnp.sum(accs[r], axis=0, keepdims=True)
            return carry

        lax.fori_loop(0, npred, body, 0, unroll=True)


def fit_chunk(wl, cov, along, off, width):
    npred, rows, _ = cov.shape
    nrow = along.shape[2]
    return pl.pallas_call(
        fit_kernel,
        grid=(width // TN,),
        in_specs=[
            pl.BlockSpec((4, H, L), lambda j: (0, 0, 0)),
            pl.BlockSpec((npred, rows, TN), lambda j: (0, 0, j + off)),
            pl.BlockSpec((npred, 1, nrow, TN), lambda j: (0, j + off, 0, 0)),
        ],
        out_specs=pl.BlockSpec((rows, TN), lambda j: (0, j)),
        out_shape=jax.ShapeDtypeStruct((rows, width), jnp.float32),
        compiler_params=pltpu.CompilerParams(dimension_semantics=("arbitrary",)),
        cost_estimate=pl.CostEstimate(
            flops=10 * npred * rows * width,
            transcendentals=0,
            bytes_accessed=2 * npred * rows * width + 4 * npred * nrow * width + 4 * rows * width,
        ),
    )(wl, cov, along)


def back_chunk(wl, cov, halves, target, land, off, nrow):
    npred, rows, _ = cov.shape
    cur, other, mine = halves
    width = cur.shape[1]
    return pl.pallas_call(
        back_kernel,
        grid=(width // TN,),
        in_specs=[
            pl.BlockSpec(memory_space=pltpu.SMEM),
            pl.BlockSpec((4, H, L), lambda j: (0, 0, 0)),
            pl.BlockSpec((npred, rows, TN), lambda j: (0, 0, j + off)),
            pl.BlockSpec((rows // 2, TN), lambda j: (0, j)),
            pl.BlockSpec((rows // 2, TN), lambda j: (0, j)),
            pl.BlockSpec((rows, TN), lambda j: (0, j + off)),
            pl.BlockSpec((rows, TN), lambda j: (0, j + off)),
        ],
        out_specs=pl.BlockSpec((npred, 1, nrow, TN), lambda j: (0, j, 0, 0)),
        out_shape=jax.ShapeDtypeStruct((npred, width // TN, nrow, TN), jnp.float32),
        scratch_shapes=[pltpu.VMEM((4, rows, L), jnp.float32)],
        compiler_params=pltpu.CompilerParams(dimension_semantics=("arbitrary",)),
        cost_estimate=pl.CostEstimate(
            flops=10 * npred * rows * width,
            transcendentals=0,
            bytes_accessed=2 * npred * rows * width + 12 * rows * width + 4 * npred * nrow * width,
        ),
    )(mine, wl, cov, cur, other, target, land)


def penalty(padded, count):
    stencil = [1.0, -4.0, 6.0, -4.0, 1.0]
    along_rows = None
    for ii in range(5):
        term = stencil[ii] * padded[..., ii : ii + count, :]
        along_rows = term if along_rows is None else along_rows + term
    centre = padded[..., 2 : count + 2, :]
    width = centre.shape[-1]
    wide = jnp.pad(centre, [(0, 0)] * (centre.ndim - 1) + [(2, 2)])
    for ii in range(5):
        along_rows = along_rows + stencil[ii] * wide[..., ii : ii + width]
    return along_rows


def local(covariates, target, land, coefs, first_moment, second_moment, smoothing):
    npred, rows, ny = covariates.shape
    count = coefs.shape[1]
    knots = coefs.shape[2]
    share = rows // lax.axis_size("pred")
    start = lax.axis_index("pred") * share
    wl = jnp.broadcast_to(weight_table(H)[:, :, None], (4, H, L))
    padded = extended(coefs, (("tile", 1),), 2)
    along = banded_along(padded, ny)
    nrow = padded.shape[1]
    target_blk = lax.dynamic_slice_in_dim(target, start, share, 0)
    land_blk = lax.dynamic_slice_in_dim(land, start, share, 0).astype(jnp.float32)
    blocks = ny // TN
    base = blocks // CHUNKS
    counts = [base] * CHUNKS
    if base >= 2 and CHUNKS >= 2 and blocks == base * CHUNKS:
        counts[0] -= 1
        counts[-1] += 1
    offs = [sum(counts[:c]) for c in range(CHUNKS)]
    widths = [n * TN for n in counts]
    width = widths[0]
    steps = reduce_steps(jnp.zeros((rows, width), jnp.float32), "pred")
    bit0 = lax.axis_index("pred") % 2
    bits_arr = jnp.reshape(bit0, (1,)).astype(jnp.int32)

    def attach(halves):
        return (halves[0], halves[1], bits_arr)

    nsteps = len(steps)
    state = [None] * CHUNKS
    fitted_parts = [None] * CHUNKS
    back_parts = [None] * CHUNKS
    state[0] = fit_chunk(wl, covariates, along, offs[0], widths[0])
    next_back = 0
    for s in range(1, CHUNKS + nsteps + 1):
        pending = []
        for c in range(CHUNKS):
            k = s - c - 1
            if 0 <= k < nsteps:
                _, fn, pairs = steps[k]
                send, finish = fn(state[c])
                pending.append((c, finish, lax.ppermute(send, "pred", pairs)))
        outs = []
        if s < CHUNKS:
            outs.append(("fit", s, fit_chunk(wl, covariates, along, offs[s], widths[s])))
        if next_back < CHUNKS and next_back + nsteps + 1 <= s:
            c = next_back
            state[c] = attach(state[c])
            outs.append(("back", c, back_chunk(wl, covariates, state[c], target, land, offs[c], nrow)))
            next_back += 1
        recvs = [r for _, _, r in pending]
        if outs:
            recvs, vals = lax.optimization_barrier((recvs, [v for _, _, v in outs]))
            for (kind, c, _), v in zip(outs, vals):
                if kind == "fit":
                    state[c] = v
                else:
                    back_parts[c] = v
        for (c, finish, _), r in zip(pending, recvs):
            state[c] = finish(r)
    for c in range(CHUNKS):
        if back_parts[c] is None:
            state[c] = attach(state[c])
            back_parts[c] = back_chunk(wl, covariates, state[c], target, land, offs[c], nrow)
        cur, other, _ = state[c]
        half = rows // 2
        side = start // half
        picked = jnp.where(bit0 == side, cur, other)
        fitted_parts[c] = lax.dynamic_slice_in_dim(picked, start - side * half, share, 0)
    fitted = jnp.concatenate(fitted_parts, axis=1)
    residual = land_blk * (target_blk - fitted)
    grad_pad = -(1.0 / H) * banded_data(back_parts, knots)
    inner = grad_pad[:, 2 : count + 2]
    from_below = from_behind(grad_pad[:, count + 2 :], "tile", 1)
    from_above = from_behind(grad_pad[:, :2], "tile", -1)
    middle = jnp.zeros((inner.shape[0], count - 2, inner.shape[2]), jnp.float32)
    low_add = jnp.concatenate([from_below, middle], axis=1)
    high_add = jnp.concatenate([middle, from_above], axis=1)
    data = inner + low_add + high_add
    gradient = data + smoothing[:, None, None] * penalty(padded, count)
    new_first = 0.9 * first_moment + 0.1 * gradient
    new_second = 0.99 * second_moment + 0.01 * gradient * gradient
    new_coefs = coefs - 0.1 * new_first / (jnp.sqrt(new_second) + 1e-08)
    return (fitted, residual, gradient, new_coefs, new_first, new_second)


def solution(mesh):
    in_specs = (
        P("pred", "tile", None),
        P("tile", None),
        P("tile", None),
        P("pred", "tile", None),
        P("pred", "tile", None),
        P("pred", "tile", None),
        P("pred"),
    )
    out_specs = (
        P(("tile", "pred"), None),
        P(("tile", "pred"), None),
        P("pred", "tile", None),
        P("pred", "tile", None),
        P("pred", "tile", None),
        P("pred", "tile", None),
    )
    return jax.shard_map(local, mesh=mesh, in_specs=in_specs, out_specs=out_specs, check_vma=False)
```
